128 devices in a mesh: iface: 4 (over x), sub: 32 (over y, z, core).
Axes of the slice: x: 4, y: 4, z: 4, core: 2. Of those that a mesh axis runs over, the one named last changes fastest.
Arguments:
- schur_blocks: bfloat16 [2048, 512, 512], P('sub', 'iface'), as said below
- noise_field: float32 [32, 2048, 512], P(None, 'sub', 'iface')
- peer_device: int32 [2048, 512], P('sub', 'iface'), may hold values from 0 to 127, as said below
- partner_slot: int32 [2048, 512], P('sub', 'iface'), may hold values from 0 to 8191, as said below
- pivot_rows: int32 [32], replicated, may hold values from 0 to 1048575
Outputs:
- constraints: float32 [32, 2048, 512], P(None, 'sub', 'iface')
The draws below stay inside these ranges and needn't reach their ends.
Inputs may be any that keep to these rules, and one draw needn't show every extreme that they name: `schur_blocks`: each block is exactly symmetric and positive definite. Devices are numbered iface index times the size of sub plus sub index; a device's dofs are numbered local subdomain * 128 + dof within its group. If peer_device names the holding device, the partner is that device's dof number partner_slot. Otherwise the partner is the dof of device peer_device that names this device with the same partner_slot, which is then below 64. Two devices share at most 64 pairs, and exactly 64 in every draw for some two devices. The relation is symmetric. `partner_slot`: see peer_device.
All inputs are finite; a program needn't handle non-finite values.
Results may differ from the reference program's by a relative error of at most 0.0071.
Values may be sent and summed in bfloat16 or wider, within the bound.
No kernel may reach another device: no remote copies, remote signals or barrier semaphores. Data moves between devices by JAX's collectives and lax.ppermute only.
A program may use at most 128 MiB of HBM per device.

```python
import math
import jax
import jax.numpy as jnp
from jax import lax

D = 512
K = 32
SUB_DEV = 64
DOFS = 1048576
N_IFACE = 4
N_SUB = 32


def arrange_rows(values):
    group = D // N_IFACE
    shaped = values.reshape(N_IFACE, N_SUB, SUB_DEV, group)
    return shaped.transpose(1, 2, 0, 3).reshape(N_SUB * SUB_DEV, D)


def pairing_tables(base_key):
    device_count = N_IFACE * N_SUB
    group = D // N_IFACE
    per_device = SUB_DEV * group
    capacity = per_device // device_count
    key_level, key_order, key_rows = jax.random.split(jax.random.fold_in(base_key, 4242), 3)
    levels = jax.random.randint(key_level, (device_count,), 6, 17)
    device_order = jax.random.permutation(key_order, device_count)
    levels = levels.at[device_order[0]].set(16).at[device_order[1]].set(16)
    counts = 2 * (capacity // 2 * levels[:, None] * levels[None, :] // 256)
    counts = counts * (1 - jnp.eye(device_count, dtype=jnp.int32))
    bounds = jnp.cumsum(counts, axis=1).astype(jnp.int32)
    starts = bounds - counts
    crossing_total = bounds[:, -1]
    self_total = per_device - crossing_total
    position = jnp.arange(per_device, dtype=jnp.int32)
    block_found = jax.vmap(lambda edge_row: jnp.searchsorted(edge_row, position, side='right'))(bounds).astype(jnp.int32)
    device_ids = jnp.arange(device_count, dtype=jnp.int32)[:, None]
    crossing = position[None, :] < crossing_total[:, None]
    peer_sorted = jnp.where(crossing, block_found, device_ids)
    block_start = jnp.take_along_axis(starts, jnp.minimum(block_found, device_count - 1), axis=1)
    slot_sorted = position[None, :] - block_start
    own_offset = position[None, :] - crossing_total[:, None]
    half_self = self_total[:, None] // 2
    mate_offset = jnp.where(own_offset < half_self, own_offset + half_self, own_offset - half_self)
    mate_sorted = jnp.clip(crossing_total[:, None] + mate_offset, 0, per_device - 1)
    row_keys = jax.random.split(key_rows, device_count)
    layout = jax.vmap(lambda one_key: jax.random.permutation(one_key, per_device))(row_keys).astype(jnp.int32)
    inverse = jnp.argsort(layout, axis=1).astype(jnp.int32)
    mate_row = jnp.take_along_axis(layout, mate_sorted, axis=1)
    slot_final = jnp.where(crossing, slot_sorted, mate_row)
    peer_rows = jnp.take_along_axis(peer_sorted, inverse, axis=1)
    slot_rows = jnp.take_along_axis(slot_final, inverse, axis=1)
    return (arrange_rows(peer_rows), arrange_rows(slot_rows))


def draw_peer_device(key, part):
    return pairing_tables(key)[0]


def draw_partner_slot(key, part):
    return pairing_tables(key)[1]


def draw_schur_blocks(key, part):
    block_keys = jax.random.split(jax.random.fold_in(key, 77), SUB_DEV * N_SUB)
    identity = jnp.eye(D, dtype=jnp.float32)

    def one_block(block_key):
        key_off, key_diag = jax.random.split(block_key)
        entries = jax.random.normal(key_off, (D, D), jnp.float32)
        diagonal = jax.random.uniform(key_diag, (D,), jnp.float32, 1.0, 2.0)
        mixed = (entries + entries.T) * (0.4 / math.sqrt(2.0 * D))
        return (mixed * (1.0 - identity) + identity * diagonal[None, :]).astype(jnp.bfloat16)
    return lax.map(one_block, block_keys)


def draw_noise_field(key, part):
    key_main, key_rough = jax.random.split(jax.random.fold_in(key, 91), 2)
    total_subs = SUB_DEV * N_SUB
    stepping = jnp.arange(total_subs, dtype=jnp.float32)[None, :, None] / total_subs
    rough = jnp.exp(jax.random.uniform(key_rough, (1, total_subs, D), jnp.float32, -0.7, 0.7))
    values = jax.random.normal(key_main, (K, total_subs, D), jnp.float32)
    ramp_scale = 0.5 + stepping
    return values * ramp_scale * rough


def touch_ends(values, rng, low, high):
    spot = [jax.random.randint(jax.random.fold_in(rng, axis), (), 0, length) for axis, length in enumerate(values.shape)]
    longest = values.shape.index(max(values.shape))
    neighbour = spot[:longest] + [(spot[longest] + 1) % values.shape[longest]] + spot[longest + 1:]
    return values.at[tuple(spot)].set(low).at[tuple(neighbour)].set(high)


def setup_inputs(seed: int = 0) -> dict:
    streams_of = jax.random.split(jax.random.key(seed), 6)
    return {
        "schur_blocks": draw_schur_blocks(jax.random.fold_in(streams_of[5], 71), 0),
        "noise_field": draw_noise_field(jax.random.fold_in(streams_of[5], 71), 0),
        "peer_device": draw_peer_device(jax.random.fold_in(streams_of[5], 71), 0),
        "partner_slot": draw_partner_slot(jax.random.fold_in(streams_of[5], 71), 0),
        "pivot_rows": touch_ends(jax.random.randint(streams_of[4], (K,), 0, DOFS), jax.random.fold_in(streams_of[4], 1), 0, DOFS - 1).astype(jnp.int32),
    }


def to_device_rows(values):
    group = D // N_IFACE
    leading = values.shape[0]
    shaped = values.reshape(leading, N_SUB, SUB_DEV, N_IFACE, group)
    return shaped.transpose(0, 3, 1, 2, 4).reshape(leading, N_IFACE * N_SUB * SUB_DEV * group)

def from_device_rows(values):
    group = D // N_IFACE
    leading = values.shape[0]
    shaped = values.reshape(leading, N_IFACE, N_SUB, SUB_DEV, group)
    return shaped.transpose(0, 2, 3, 1, 4).reshape(leading, N_SUB * SUB_DEV, D)

def partner_index(peer_device, partner_slot):
    device_count = N_IFACE * N_SUB
    group = D // N_IFACE
    per_device = SUB_DEV * group
    capacity = per_device // device_count
    peer_rows = to_device_rows(peer_device[None])[0].reshape(device_count, per_device)
    slot_rows = to_device_rows(partner_slot[None])[0].reshape(device_count, per_device)
    owner = jnp.arange(device_count, dtype=jnp.int32)[:, None]
    crossing = peer_rows != owner
    global_row = owner * per_device + jnp.arange(per_device, dtype=jnp.int32)[None, :]
    table_size = device_count * device_count * capacity
    own_key = jnp.where(crossing, (owner * device_count + peer_rows) * capacity + slot_rows, table_size)
    lookup_table = jnp.zeros((table_size,), jnp.int32).at[own_key.reshape(-1)].set(global_row.reshape(-1), mode='drop')
    mate_key = jnp.where(crossing, (peer_rows * device_count + owner) * capacity + slot_rows, 0)
    far_row = jnp.take(lookup_table, mate_key)
    near_row = owner * per_device + slot_rows
    return jnp.where(crossing, far_row, near_row).reshape(-1).astype(jnp.int32)

def jump_field(values, partner):
    flattened = to_device_rows(values)
    return from_device_rows(flattened - jnp.take(flattened, partner, axis=1))

def apply_blocks(vector_half, schur_blocks):
    count_groups = schur_blocks.shape[0] // SUB_DEV
    stacked = schur_blocks.reshape(count_groups, SUB_DEV, D, D)
    pieces = vector_half.reshape(K, count_groups, SUB_DEV, D).transpose(1, 0, 2, 3)

    def one_group(pair_in):
        block_part, vector_part = pair_in
        return jnp.einsum('ksc,src->ksr', vector_part.astype(jnp.float32), block_part.astype(jnp.float32), precision=lax.Precision.HIGHEST)
    result = lax.map(one_group, (stacked, pieces))
    return result.transpose(1, 0, 2, 3).reshape(K, count_groups * SUB_DEV, D)

def combine_weights(gram_matrix, picked, total_rows):
    lower = jnp.linalg.cholesky(gram_matrix)
    solved = jax.scipy.linalg.cho_solve((lower, True), picked)
    coupling = jnp.dot(picked.T, solved, precision=lax.Precision.HIGHEST) * (total_rows / K) + jnp.eye(K, dtype=jnp.float32)
    lower_two = jnp.linalg.cholesky(coupling)
    return jax.scipy.linalg.cho_solve((lower_two, True), solved.T) * (total_rows / math.sqrt(K))

def reference(schur_blocks, noise_field, peer_device, partner_slot, pivot_rows):
    partner = partner_index(peer_device, partner_slot)
    first_jump = jump_field(noise_field, partner)
    first_half = first_jump.astype(jnp.bfloat16)
    second_jump = jump_field(apply_blocks(first_half, schur_blocks), partner)
    second_half = second_jump.astype(jnp.bfloat16)
    samples = jump_field(apply_blocks(second_half, schur_blocks), partner)
    flattened = samples.reshape(K, -1)
    gram_matrix = lax.dot_general(flattened.astype(jnp.float32), flattened.astype(jnp.float32), (((1,), (1,)), ((), ())), precision=lax.Precision.HIGHEST, preferred_element_type=jnp.float32)
    picked = jnp.take(flattened, pivot_rows, axis=1)
    coefficients = combine_weights(gram_matrix, picked, float(N_SUB * SUB_DEV * D))
    constraint_rows = jnp.dot(coefficients.astype(jnp.float32), flattened.astype(jnp.float32), precision=lax.Precision.HIGHEST, preferred_element_type=jnp.float32)
    return constraint_rows.reshape(K, N_SUB * SUB_DEV, D)
```

```python
import math

import jax
import jax.numpy as jnp
from jax import lax
from jax.experimental import pallas as pl
from jax.experimental.pallas import tpu as pltpu
from jax.sharding import PartitionSpec as P

UNROLL = 16


def _pack_kernel(slot_ref, x_ref, o_ref, buf):
    buf[...] = jnp.zeros_like(buf)

    def body(j, carry):
        for u in range(UNROLL):
            i = j * UNROLL + u
            buf[pl.ds(slot_ref[i], 1), :] = x_ref[pl.ds(i, 1), :]
        return carry

    lax.fori_loop(0, x_ref.shape[0] // UNROLL, body, 0)
    o_ref[...] = buf[pl.ds(0, o_ref.shape[0]), :]


def _unpack_kernel(src_ref, v_ref, inc_ref, o_ref, joined, picked):
    rows = v_ref.shape[0]
    joined[pl.ds(0, rows), :] = v_ref[...]
    joined[pl.ds(rows, rows), :] = inc_ref[...]

    def body(j, carry):
        for u in range(UNROLL):
            q = j * UNROLL + u
            picked[pl.ds(q, 1), :] = joined[pl.ds(src_ref[q], 1), :]
        return carry

    lax.fori_loop(0, rows // UNROLL, body, 0)
    o_ref[...] = v_ref[...] - picked[...]


def pack_rows(x, send_pos):
    rows, width = x.shape
    return pl.pallas_call(
        _pack_kernel,
        in_specs=[pl.BlockSpec(memory_space=pltpu.SMEM), pl.BlockSpec(memory_space=pltpu.VMEM)],
        out_specs=pl.BlockSpec(memory_space=pltpu.VMEM),
        out_shape=jax.ShapeDtypeStruct((rows, width), x.dtype),
        scratch_shapes=[pltpu.VMEM((rows + 8, width), x.dtype)],
        compiler_params=pltpu.CompilerParams(vmem_limit_bytes=48 * 1024 * 1024),
    )(send_pos, x)


def unpack_jump(v, incoming, source):
    rows, width = v.shape
    return pl.pallas_call(
        _unpack_kernel,
        in_specs=[
            pl.BlockSpec(memory_space=pltpu.SMEM),
            pl.BlockSpec(memory_space=pltpu.VMEM),
            pl.BlockSpec(memory_space=pltpu.VMEM),
        ],
        out_specs=pl.BlockSpec(memory_space=pltpu.VMEM),
        out_shape=jax.ShapeDtypeStruct((rows, width), v.dtype),
        scratch_shapes=[
            pltpu.VMEM((2 * rows, width), v.dtype),
            pltpu.VMEM((rows, width), v.dtype),
        ],
        compiler_params=pltpu.CompilerParams(vmem_limit_bytes=48 * 1024 * 1024),
    )(source, v, incoming)


def partner_jump(rows_in, routing, device_count):
    send_pos, source = routing
    rows, width = rows_in.shape
    outgoing = pack_rows(rows_in, send_pos)
    exchanged = lax.all_to_all(
        outgoing.reshape(device_count, rows // device_count * width),
        ("iface", "sub"),
        split_axis=0,
        concat_axis=0,
        tiled=True,
    )
    incoming = exchanged.reshape(rows, width)
    return unpack_jump(rows_in, incoming, source)


def apply_blocks(jump_rows, schur_blocks, sub_local, group):
    width = jump_rows.shape[1]
    half = jump_rows.astype(jnp.bfloat16).reshape(sub_local, group, width).transpose(2, 0, 1)
    gathered = lax.all_gather(half, "iface", axis=2, tiled=True)
    result = jnp.einsum("src,ksc->srk", schur_blocks, gathered, preferred_element_type=jnp.float32)
    return result.reshape(sub_local * group, width)


def combine_weights(gram_matrix, picked, total_rows, sample_count):
    lower = jnp.linalg.cholesky(gram_matrix)
    solved = jax.scipy.linalg.cho_solve((lower, True), picked)
    coupling = jnp.dot(picked.T, solved, precision=lax.Precision.HIGHEST) * (
        total_rows / sample_count
    ) + jnp.eye(sample_count, dtype=jnp.float32)
    lower_two = jnp.linalg.cholesky(coupling)
    return jax.scipy.linalg.cho_solve((lower_two, True), solved.T) * (
        total_rows / math.sqrt(sample_count)
    )


def shards(schur_blocks, noise_field, peer_device, partner_slot, pivot_rows):
    sample_count, sub_local, group = noise_field.shape
    row_count = sub_local * group
    iface_count = lax.axis_size("iface")
    sub_count = lax.axis_size("sub")
    device_count = iface_count * sub_count
    capacity = row_count // device_count
    full_width = group * iface_count
    iface_place = lax.axis_index("iface")
    sub_place = lax.axis_index("sub")
    device_self = iface_place * sub_count + sub_place
    peer_flat = peer_device.reshape(row_count)
    slot_flat = partner_slot.reshape(row_count)
    crossing = peer_flat != device_self
    send_pos = jnp.clip(
        jnp.where(crossing, peer_flat * capacity + slot_flat, row_count), 0, row_count
    ).astype(jnp.int32)
    source = jnp.clip(
        jnp.where(crossing, row_count + peer_flat * capacity + slot_flat, slot_flat),
        0,
        2 * row_count - 1,
    ).astype(jnp.int32)
    routing = (send_pos, source)
    noise_rows = noise_field.transpose(1, 2, 0).reshape(row_count, sample_count)
    first_jump = partner_jump(noise_rows, routing, device_count)
    response_one = apply_blocks(first_jump, schur_blocks, sub_local, group)
    second_jump = partner_jump(response_one, routing, device_count)
    response_two = apply_blocks(second_jump, schur_blocks, sub_local, group)
    samples = partner_jump(response_two, routing, device_count)
    gram_part = lax.dot_general(
        samples,
        samples,
        (((0,), (0,)), ((), ())),
        precision=lax.Precision.HIGHEST,
        preferred_element_type=jnp.float32,
    )
    pivot_sub = pivot_rows // full_width
    pivot_dof = pivot_rows % full_width
    holder = (pivot_sub // sub_local == sub_place) & (pivot_dof // group == iface_place)
    local_row = pivot_sub % sub_local * group + pivot_dof % group
    picked_part = jnp.take(samples, local_row, axis=0, mode="clip").T * holder[None, :].astype(
        jnp.float32
    )
    partial = jnp.concatenate((gram_part, picked_part), axis=1)[None]
    over_sub = jnp.sum(lax.all_gather(partial, "sub", axis=0, tiled=True), axis=0, keepdims=True)
    total = jnp.sum(lax.all_gather(over_sub, "iface", axis=0, tiled=True), axis=0)
    gram_matrix = total[:, :sample_count]
    picked = total[:, sample_count:]
    total_rows = float(sub_local * sub_count * full_width)
    coefficients = combine_weights(gram_matrix, picked, total_rows, sample_count)
    constraint_rows = lax.dot_general(
        coefficients,
        samples,
        (((1,), (1,)), ((), ())),
        precision=lax.Precision.HIGHEST,
        preferred_element_type=jnp.float32,
    )
    return constraint_rows.reshape(sample_count, sub_local, group)


def solution(mesh):
    placed = (
        P("sub", "iface", None),
        P(None, "sub", "iface"),
        P("sub", "iface"),
        P("sub", "iface"),
        P(),
    )
    return jax.shard_map(
        shards, mesh=mesh, in_specs=placed, out_specs=P(None, "sub", "iface"), check_vma=False
    )
```

```python
import math

import jax
import jax.numpy as jnp
from jax import lax
from jax.experimental import pallas as pl
from jax.experimental.pallas import tpu as pltpu
from jax.sharding import PartitionSpec as P

UNROLL = 16


def _pack_kernel(slot_ref, x_ref, o_ref, buf):
    rows = x_ref.shape[0]
    buf[...] = jnp.zeros_like(buf)
    def body(j, carry):
        for u in range(UNROLL):
            i = j * UNROLL + u
            buf[pl.ds(slot_ref[i], 1), :] = x_ref[pl.ds(i, 1), :]
        return carry
    lax.fori_loop(0, rows // UNROLL, body, 0)
    width = x_ref.shape[1]
    per = o_ref.shape[1] // width
    n = o_ref.shape[0]
    lane = lax.broadcasted_iota(jnp.int32, (n, o_ref.shape[1]), 1) // width
    acc = jnp.zeros((n, o_ref.shape[1]), jnp.float32)
    for t in range(per):
        piece = buf[pl.ds(t, n, stride=per), :]
        wide = jnp.concatenate([piece] + [jnp.zeros_like(piece)] * (per - 1), axis=1)
        if t:
            wide = pltpu.roll(wide, shift=width * t, axis=1)
        acc = jnp.where(lane == t, wide, acc)
    o_ref[...] = acc

def _unpack_kernel(src_ref, v_ref, inc_ref, o_ref, joined, picked):
    rows, width = v_ref.shape
    n, lanes = inc_ref.shape
    per = lanes // width
    joined[pl.ds(0, rows), :] = v_ref[...]
    inc = inc_ref[...]
    for t in range(per):
        part = inc if t == 0 else pltpu.roll(inc, shift=lanes - width * t, axis=1)
        joined[pl.ds(rows + t, n, stride=per), :] = part[:, :width]
    def body(j, carry):
        for u in range(UNROLL):
            q = j * UNROLL + u
            picked[pl.ds(q, 1), :] = joined[pl.ds(src_ref[q], 1), :]
        return carry
    lax.fori_loop(0, rows // UNROLL, body, 0)
    o_ref[...] = v_ref[...] - picked[...]

def pack_rows(x, send_pos):
    rows, width = x.shape
    return pl.pallas_call(_pack_kernel,
        in_specs=[pl.BlockSpec(memory_space=pltpu.SMEM), pl.BlockSpec(memory_space=pltpu.VMEM)],
        out_specs=pl.BlockSpec(memory_space=pltpu.VMEM),
        out_shape=jax.ShapeDtypeStruct((rows * width // 128, 128), x.dtype),
        scratch_shapes=[pltpu.VMEM((rows + 8, width), x.dtype)],
        compiler_params=pltpu.CompilerParams(vmem_limit_bytes=48 * 1024 * 1024))(send_pos, x)

def unpack_jump(v, incoming, source):
    rows, width = v.shape
    return pl.pallas_call(_unpack_kernel,
        in_specs=[pl.BlockSpec(memory_space=pltpu.SMEM), pl.BlockSpec(memory_space=pltpu.VMEM), pl.BlockSpec(memory_space=pltpu.VMEM)],
        out_specs=pl.BlockSpec(memory_space=pltpu.VMEM),
        out_shape=jax.ShapeDtypeStruct((rows, width), v.dtype),
        scratch_shapes=[pltpu.VMEM((2 * rows, width), v.dtype), pltpu.VMEM((rows, width), v.dtype)],
        compiler_params=pltpu.CompilerParams(vmem_limit_bytes=48 * 1024 * 1024))(source, v, incoming)


def partner_jump(rows_in, routing, device_count):
    send_pos, source = routing
    outgoing = pack_rows(rows_in, send_pos)
    incoming = lax.all_to_all(outgoing, ("iface", "sub"), split_axis=0, concat_axis=0, tiled=True)
    return unpack_jump(rows_in, incoming, source)


def apply_blocks(jump_rows, schur_blocks, sub_local, group):
    width = jump_rows.shape[1]
    half = jump_rows.astype(jnp.bfloat16).reshape(sub_local, group, width).transpose(2, 0, 1)
    gathered = lax.all_gather(half, "iface", axis=2, tiled=True)
    result = jnp.einsum("src,ksc->srk", schur_blocks, gathered, preferred_element_type=jnp.float32)
    return result.reshape(sub_local * group, width)


def combine_weights(gram_matrix, picked, total_rows, sample_count):
    lower = jnp.linalg.cholesky(gram_matrix)
    solved = jax.scipy.linalg.cho_solve((lower, True), picked)
    coupling = jnp.dot(picked.T, solved, precision=lax.Precision.HIGHEST) * (
        total_rows / sample_count
    ) + jnp.eye(sample_count, dtype=jnp.float32)
    lower_two = jnp.linalg.cholesky(coupling)
    return jax.scipy.linalg.cho_solve((lower_two, True), solved.T) * (
        total_rows / math.sqrt(sample_count)
    )


def shards(schur_blocks, noise_field, peer_device, partner_slot, pivot_rows):
    sample_count, sub_local, group = noise_field.shape
    row_count = sub_local * group
    iface_count = lax.axis_size("iface")
    sub_count = lax.axis_size("sub")
    device_count = iface_count * sub_count
    capacity = row_count // device_count
    full_width = group * iface_count
    iface_place = lax.axis_index("iface")
    sub_place = lax.axis_index("sub")
    device_self = iface_place * sub_count + sub_place
    peer_flat = peer_device.reshape(row_count)
    slot_flat = partner_slot.reshape(row_count)
    crossing = peer_flat != device_self
    send_pos = jnp.clip(
        jnp.where(crossing, peer_flat * capacity + slot_flat, row_count), 0, row_count
    ).astype(jnp.int32)
    source = jnp.clip(
        jnp.where(crossing, row_count + peer_flat * capacity + slot_flat, slot_flat),
        0,
        2 * row_count - 1,
    ).astype(jnp.int32)
    routing = (send_pos, source)
    noise_rows = noise_field.transpose(1, 2, 0).reshape(row_count, sample_count)
    first_jump = partner_jump(noise_rows, routing, device_count)
    response_one = apply_blocks(first_jump, schur_blocks, sub_local, group)
    second_jump = partner_jump(response_one, routing, device_count)
    response_two = apply_blocks(second_jump, schur_blocks, sub_local, group)
    samples = partner_jump(response_two, routing, device_count)
    gram_part = lax.dot_general(
        samples,
        samples,
        (((0,), (0,)), ((), ())),
        precision=lax.Precision.HIGHEST,
        preferred_element_type=jnp.float32,
    )
    pivot_sub = pivot_rows // full_width
    pivot_dof = pivot_rows % full_width
    holder = (pivot_sub // sub_local == sub_place) & (pivot_dof // group == iface_place)
    local_row = pivot_sub % sub_local * group + pivot_dof % group
    picked_part = jnp.take(samples, local_row, axis=0, mode="clip").T * holder[None, :].astype(
        jnp.float32
    )
    partial = jnp.concatenate((gram_part, picked_part), axis=1)[None]
    over_sub = jnp.sum(lax.all_gather(partial, "sub", axis=0, tiled=True), axis=0, keepdims=True)
    total = jnp.sum(lax.all_gather(over_sub, "iface", axis=0, tiled=True), axis=0)
    gram_matrix = total[:, :sample_count]
    picked = total[:, sample_count:]
    total_rows = float(sub_local * sub_count * full_width)
    coefficients = combine_weights(gram_matrix, picked, total_rows, sample_count)
    constraint_rows = lax.dot_general(
        coefficients,
        samples,
        (((1,), (1,)), ((), ())),
        precision=lax.Precision.HIGHEST,
        preferred_element_type=jnp.float32,
    )
    return constraint_rows.reshape(sample_count, sub_local, group)


def solution(mesh):
    placed = (
        P("sub", "iface", None),
        P(None, "sub", "iface"),
        P("sub", "iface"),
        P("sub", "iface"),
        P(),
    )
    return jax.shard_map(
        shards, mesh=mesh, in_specs=placed, out_specs=P(None, "sub", "iface"), check_vma=False
    )
```

```python
import functools
import math

import jax
import jax.numpy as jnp
from jax import lax
from jax.experimental import pallas as pl
from jax.experimental.pallas import tpu as pltpu
from jax.sharding import PartitionSpec as P

UNROLL = 32
PIECES = 2


def _pack_kernel(slot_ref, *refs):
    x_refs, o_ref, buf = refs[:-2], refs[-2], refs[-1]
    buf[...] = jnp.zeros_like(buf)
    offset = 0
    for x_ref in x_refs:
        def body(j, carry, x_ref=x_ref, offset=offset):
            base = pl.multiple_of(j * UNROLL, UNROLL)
            for u in range(UNROLL):
                buf[pl.ds(slot_ref[offset + base + u], 1), :] = x_ref[pl.ds(base + u, 1), :]
            return carry

        lax.fori_loop(0, x_ref.shape[0] // UNROLL, body, 0)
        offset += x_ref.shape[0]
    width = buf.shape[1]
    n, lanes = o_ref.shape
    per = lanes // width
    lane = lax.broadcasted_iota(jnp.int32, (n, lanes), 1) // width
    acc = jnp.zeros((n, lanes), jnp.float32)
    for t in range(per):
        piece = buf[pl.ds(t, n, stride=per), :]
        wide = jnp.concatenate([piece] + [jnp.zeros_like(piece)] * (per - 1), axis=1)
        if t:
            wide = pltpu.roll(wide, shift=width * t, axis=1)
        acc = jnp.where(lane == t, wide, acc)
    o_ref[...] = acc


def _unpack_kernel(first, count, src_ref, *refs):
    v_refs, inc_ref, o_ref, joined, picked = refs[:-4], refs[-4], refs[-3], refs[-2], refs[-1]
    rows = sum(v_ref.shape[0] for v_ref in v_refs)
    width = v_refs[0].shape[1]
    n, lanes = inc_ref.shape
    per = lanes // width
    offset = 0
    for v_ref in v_refs:
        joined[pl.ds(offset, v_ref.shape[0]), :] = v_ref[...]
        offset += v_ref.shape[0]
    inc = inc_ref[...]
    for t in range(per):
        part = inc if t == 0 else pltpu.roll(inc, shift=lanes - width * t, axis=1)
        joined[pl.ds(rows + t, n, stride=per), :] = part[:, :width]

    def body(j, carry):
        base = pl.multiple_of(j * UNROLL, UNROLL)
        for u in range(UNROLL):
            picked[pl.ds(base + u, 1), :] = joined[pl.ds(src_ref[first + base + u], 1), :]
        return carry

    lax.fori_loop(0, count // UNROLL, body, 0)
    offset = 0
    for v_ref in v_refs:
        low = max(offset, first)
        high = min(offset + v_ref.shape[0], first + count)
        if low < high:
            o_ref[pl.ds(low - first, high - low), :] = (
                v_ref[pl.ds(low - offset, high - low), :] - picked[pl.ds(low - first, high - low), :]
            )
        offset += v_ref.shape[0]


def pack_rows(xs, send_pos):
    rows = sum(x.shape[0] for x in xs)
    width = xs[0].shape[1]
    return pl.pallas_call(
        _pack_kernel,
        in_specs=[pl.BlockSpec(memory_space=pltpu.SMEM)]
        + [pl.BlockSpec(memory_space=pltpu.VMEM)] * len(xs),
        out_specs=pl.BlockSpec(memory_space=pltpu.VMEM),
        out_shape=jax.ShapeDtypeStruct((rows * width // 128, 128), xs[0].dtype),
        scratch_shapes=[pltpu.VMEM((rows + 8, width), xs[0].dtype)],
        compiler_params=pltpu.CompilerParams(vmem_limit_bytes=48 * 1024 * 1024),
    )(send_pos, *xs)


def unpack_jump(vs, incoming, source, first, count):
    rows = sum(v.shape[0] for v in vs)
    width = vs[0].shape[1]
    return pl.pallas_call(
        functools.partial(_unpack_kernel, first, count),
        in_specs=[pl.BlockSpec(memory_space=pltpu.SMEM)]
        + [pl.BlockSpec(memory_space=pltpu.VMEM)] * (len(vs) + 1),
        out_specs=pl.BlockSpec(memory_space=pltpu.VMEM),
        out_shape=jax.ShapeDtypeStruct((count, width), vs[0].dtype),
        scratch_shapes=[
            pltpu.VMEM((2 * rows, width), vs[0].dtype),
            pltpu.VMEM((count, width), vs[0].dtype),
        ],
        compiler_params=pltpu.CompilerParams(vmem_limit_bytes=48 * 1024 * 1024),
    )(source, *vs, incoming)


def exchange(parts, send_pos):
    outgoing = pack_rows(parts, send_pos)
    return lax.all_to_all(outgoing, ("iface", "sub"), split_axis=0, concat_axis=0, tiled=True)


def apply_blocks(jump_rows, schur_blocks, sub_local, group):
    width = jump_rows.shape[1]
    count = jump_rows.shape[0] // group
    half = jump_rows.astype(jnp.bfloat16).reshape(count, group, width).transpose(2, 0, 1)
    gathered = lax.all_gather(half, "iface", axis=2, tiled=True)
    result = jnp.einsum("src,ksc->srk", schur_blocks, gathered, preferred_element_type=jnp.float32)
    return result.reshape(count * group, width)


def jump_and_apply(parts, routing, schur_blocks, sub_local, group, pieces):
    send_pos, source = routing
    incoming = exchange(parts, send_pos)
    rows = sum(part.shape[0] for part in parts)
    step = rows // pieces
    sub_step = sub_local // pieces
    out = []
    for h in range(pieces):
        jumped = unpack_jump(parts, incoming, source, h * step, step)
        out.append(
            apply_blocks(jumped, schur_blocks[h * sub_step:(h + 1) * sub_step], sub_step, group)
        )
    return out


def combine_weights(gram_matrix, picked, total_rows, sample_count):
    lower = jnp.linalg.cholesky(gram_matrix)
    solved = jax.scipy.linalg.cho_solve((lower, True), picked)
    coupling = jnp.dot(picked.T, solved, precision=lax.Precision.HIGHEST) * (
        total_rows / sample_count
    ) + jnp.eye(sample_count, dtype=jnp.float32)
    lower_two = jnp.linalg.cholesky(coupling)
    return jax.scipy.linalg.cho_solve((lower_two, True), solved.T) * (
        total_rows / math.sqrt(sample_count)
    )


def shards(schur_blocks, noise_field, peer_device, partner_slot, pivot_rows):
    sample_count, sub_local, group = noise_field.shape
    row_count = sub_local * group
    iface_count = lax.axis_size("iface")
    sub_count = lax.axis_size("sub")
    device_count = iface_count * sub_count
    capacity = row_count // device_count
    full_width = group * iface_count
    iface_place = lax.axis_index("iface")
    sub_place = lax.axis_index("sub")
    device_self = iface_place * sub_count + sub_place
    peer_flat = peer_device.reshape(row_count)
    slot_flat = partner_slot.reshape(row_count)
    crossing = peer_flat != device_self
    send_pos = jnp.clip(
        jnp.where(crossing, peer_flat * capacity + slot_flat, row_count), 0, row_count
    ).astype(jnp.int32)
    source = jnp.clip(
        jnp.where(crossing, row_count + peer_flat * capacity + slot_flat, slot_flat),
        0,
        2 * row_count - 1,
    ).astype(jnp.int32)
    routing = (send_pos, source)
    noise_rows = noise_field.transpose(1, 2, 0).reshape(row_count, sample_count)
    response_one = jump_and_apply([noise_rows], routing, schur_blocks, sub_local, group, PIECES)
    response_two = jump_and_apply(response_one, routing, schur_blocks, sub_local, group, PIECES)
    incoming = exchange(response_two, send_pos)
    samples = unpack_jump(response_two, incoming, source, 0, row_count)
    gram_part = lax.dot_general(
        samples,
        samples,
        (((0,), (0,)), ((), ())),
        precision=lax.Precision.HIGHEST,
        preferred_element_type=jnp.float32,
    )
    pivot_sub = pivot_rows // full_width
    pivot_dof = pivot_rows % full_width
    holder = (pivot_sub // sub_local == sub_place) & (pivot_dof // group == iface_place)
    local_row = pivot_sub % sub_local * group + pivot_dof % group
    picked_part = jnp.take(samples, local_row, axis=0, mode="clip").T * holder[None, :].astype(
        jnp.float32
    )
    partial = jnp.concatenate((gram_part, picked_part), axis=1)[None]
    over_sub = jnp.sum(lax.all_gather(partial, "sub", axis=0, tiled=True), axis=0, keepdims=True)
    total = jnp.sum(lax.all_gather(over_sub, "iface", axis=0, tiled=True), axis=0)
    gram_matrix = total[:, :sample_count]
    picked = total[:, sample_count:]
    total_rows = float(sub_local * sub_count * full_width)
    coefficients = combine_weights(gram_matrix, picked, total_rows, sample_count)
    constraint_rows = lax.dot_general(
        coefficients,
        samples,
        (((1,), (1,)), ((), ())),
        precision=lax.Precision.HIGHEST,
        preferred_element_type=jnp.float32,
    )
    return constraint_rows.reshape(sample_count, sub_local, group)


def solution(mesh):
    placed = (
        P("sub", "iface", None),
        P(None, "sub", "iface"),
        P("sub", "iface"),
        P("sub", "iface"),
        P(),
    )
    return jax.shard_map(
        shards, mesh=mesh, in_specs=placed, out_specs=P(None, "sub", "iface"), check_vma=False
    )
```

```python
import functools
import math

import jax
import jax.numpy as jnp
from jax import lax
from jax.experimental import pallas as pl
from jax.experimental.pallas import tpu as pltpu
from jax.sharding import PartitionSpec as P

UNROLL = 32


def _pack_kernel(slot_ref, *refs):
    x_refs, o_ref, buf = refs[:-2], refs[-2], refs[-1]
    buf[...] = jnp.zeros_like(buf)
    offset = 0
    for x_ref in x_refs:
        def body(j, carry, x_ref=x_ref, offset=offset):
            base = pl.multiple_of(j * UNROLL, UNROLL)
            for u in range(UNROLL):
                buf[pl.ds(slot_ref[offset + base + u], 1), :] = x_ref[pl.ds(base + u, 1), :]
            return carry

        lax.fori_loop(0, x_ref.shape[0] // UNROLL, body, 0)
        offset += x_ref.shape[0]
    width = buf.shape[1]
    n, lanes = o_ref.shape
    per = lanes // width
    lane = lax.broadcasted_iota(jnp.int32, (n, lanes), 1) // width
    acc = jnp.zeros((n, lanes), jnp.float32)
    for t in range(per):
        piece = buf[pl.ds(t, n, stride=per), :]
        wide = jnp.concatenate([piece] + [jnp.zeros_like(piece)] * (per - 1), axis=1)
        if t:
            wide = pltpu.roll(wide, shift=width * t, axis=1)
        acc = jnp.where(lane == t, wide, acc)
    o_ref[...] = acc


def _unpack_kernel(first, count, src_ref, *refs):
    v_refs, inc_ref, o_ref, joined, picked = refs[:-4], refs[-4], refs[-3], refs[-2], refs[-1]
    rows = sum(v_ref.shape[0] for v_ref in v_refs)
    width = v_refs[0].shape[1]
    n, lanes = inc_ref.shape
    per = lanes // width
    offset = 0
    for v_ref in v_refs:
        joined[pl.ds(offset, v_ref.shape[0]), :] = v_ref[...]
        offset += v_ref.shape[0]
    inc = inc_ref[...]
    for t in range(per):
        part = inc if t == 0 else pltpu.roll(inc, shift=lanes - width * t, axis=1)
        joined[pl.ds(rows + t, n, stride=per), :] = part[:, :width]

    def body(j, carry):
        base = pl.multiple_of(j * UNROLL, UNROLL)
        for u in range(UNROLL):
            picked[pl.ds(base + u, 1), :] = joined[pl.ds(src_ref[first + base + u], 1), :]
        return carry

    lax.fori_loop(0, count // UNROLL, body, 0)
    offset = 0
    for v_ref in v_refs:
        low = max(offset, first)
        high = min(offset + v_ref.shape[0], first + count)
        if low < high:
            o_ref[pl.ds(low - first, high - low), :] = (
                v_ref[pl.ds(low - offset, high - low), :] - picked[pl.ds(low - first, high - low), :]
            )
        offset += v_ref.shape[0]


def pack_rows(xs, send_pos):
    rows = sum(x.shape[0] for x in xs)
    width = xs[0].shape[1]
    return pl.pallas_call(
        _pack_kernel,
        in_specs=[pl.BlockSpec(memory_space=pltpu.SMEM)]
        + [pl.BlockSpec(memory_space=pltpu.VMEM)] * len(xs),
        out_specs=pl.BlockSpec(memory_space=pltpu.VMEM),
        out_shape=jax.ShapeDtypeStruct((rows * width // 128, 128), xs[0].dtype),
        scratch_shapes=[pltpu.VMEM((rows + 8, width), xs[0].dtype)],
        compiler_params=pltpu.CompilerParams(vmem_limit_bytes=48 * 1024 * 1024),
    )(send_pos, *xs)


def unpack_jump(vs, incoming, source, first, count):
    rows = sum(v.shape[0] for v in vs)
    width = vs[0].shape[1]
    return pl.pallas_call(
        functools.partial(_unpack_kernel, first, count),
        in_specs=[pl.BlockSpec(memory_space=pltpu.SMEM)]
        + [pl.BlockSpec(memory_space=pltpu.VMEM)] * (len(vs) + 1),
        out_specs=pl.BlockSpec(memory_space=pltpu.VMEM),
        out_shape=jax.ShapeDtypeStruct((count, width), vs[0].dtype),
        scratch_shapes=[
            pltpu.VMEM((2 * rows, width), vs[0].dtype),
            pltpu.VMEM((count, width), vs[0].dtype),
        ],
        compiler_params=pltpu.CompilerParams(vmem_limit_bytes=48 * 1024 * 1024),
    )(source, *vs, incoming)


def exchange(parts, send_pos):
    outgoing = pack_rows(parts, send_pos)
    return lax.all_to_all(outgoing, ("iface", "sub"), split_axis=0, concat_axis=0, tiled=True)


def apply_blocks(jump_rows, schur_blocks, sub_local, group):
    width = jump_rows.shape[1]
    half = jump_rows.astype(jnp.bfloat16).reshape(sub_local, group, width).transpose(2, 0, 1)
    ring = lax.axis_size("iface")
    here = lax.axis_index("iface")
    total = None
    for shift in range(ring):
        if shift:
            block = lax.ppermute(half, "iface", [(i, (i + shift) % ring) for i in range(ring)])
        else:
            block = half
        owner = (here - shift) % ring
        columns = lax.dynamic_slice_in_dim(schur_blocks, owner * group, group, axis=2)
        part = jnp.einsum("src,ksc->srk", columns, block, preferred_element_type=jnp.float32)
        total = part if total is None else total + part
    return total.reshape(sub_local * group, width)


def combine_weights(gram_matrix, picked, total_rows, sample_count):
    lower = jnp.linalg.cholesky(gram_matrix)
    solved = jax.scipy.linalg.cho_solve((lower, True), picked)
    coupling = jnp.dot(picked.T, solved, precision=lax.Precision.HIGHEST) * (
        total_rows / sample_count
    ) + jnp.eye(sample_count, dtype=jnp.float32)
    lower_two = jnp.linalg.cholesky(coupling)
    return jax.scipy.linalg.cho_solve((lower_two, True), solved.T) * (
        total_rows / math.sqrt(sample_count)
    )


def shards(schur_blocks, noise_field, peer_device, partner_slot, pivot_rows):
    sample_count, sub_local, group = noise_field.shape
    row_count = sub_local * group
    iface_count = lax.axis_size("iface")
    sub_count = lax.axis_size("sub")
    device_count = iface_count * sub_count
    capacity = row_count // device_count
    full_width = group * iface_count
    iface_place = lax.axis_index("iface")
    sub_place = lax.axis_index("sub")
    device_self = iface_place * sub_count + sub_place
    peer_flat = peer_device.reshape(row_count)
    slot_flat = partner_slot.reshape(row_count)
    crossing = peer_flat != device_self
    send_pos = jnp.clip(
        jnp.where(crossing, peer_flat * capacity + slot_flat, row_count), 0, row_count
    ).astype(jnp.int32)
    source = jnp.clip(
        jnp.where(crossing, row_count + peer_flat * capacity + slot_flat, slot_flat),
        0,
        2 * row_count - 1,
    ).astype(jnp.int32)
    routing = (send_pos, source)
    noise_rows = noise_field.transpose(1, 2, 0).reshape(row_count, sample_count)
    field = [noise_rows]
    for _ in range(2):
        incoming = exchange(field, send_pos)
        jumped = unpack_jump(field, incoming, source, 0, row_count)
        field = [apply_blocks(jumped, schur_blocks, sub_local, group)]
    incoming = exchange(field, send_pos)
    samples = unpack_jump(field, incoming, source, 0, row_count)
    gram_part = lax.dot_general(
        samples,
        samples,
        (((0,), (0,)), ((), ())),
        precision=lax.Precision.HIGHEST,
        preferred_element_type=jnp.float32,
    )
    pivot_sub = pivot_rows // full_width
    pivot_dof = pivot_rows % full_width
    holder = (pivot_sub // sub_local == sub_place) & (pivot_dof // group == iface_place)
    local_row = pivot_sub % sub_local * group + pivot_dof % group
    picked_part = jnp.take(samples, local_row, axis=0, mode="clip").T * holder[None, :].astype(
        jnp.float32
    )
    partial = jnp.concatenate((gram_part, picked_part), axis=1)[None]
    over_sub = jnp.sum(lax.all_gather(partial, "sub", axis=0, tiled=True), axis=0, keepdims=True)
    total = jnp.sum(lax.all_gather(over_sub, "iface", axis=0, tiled=True), axis=0)
    gram_matrix = total[:, :sample_count]
    picked = total[:, sample_count:]
    total_rows = float(sub_local * sub_count * full_width)
    coefficients = combine_weights(gram_matrix, picked, total_rows, sample_count)
    constraint_rows = lax.dot_general(
        coefficients,
        samples,
        (((1,), (1,)), ((), ())),
        precision=lax.Precision.HIGHEST,
        preferred_element_type=jnp.float32,
    )
    return constraint_rows.reshape(sample_count, sub_local, group)


def solution(mesh):
    placed = (
        P("sub", "iface", None),
        P(None, "sub", "iface"),
        P("sub", "iface"),
        P("sub", "iface"),
        P(),
    )
    return jax.shard_map(
        shards, mesh=mesh, in_specs=placed, out_specs=P(None, "sub", "iface"), check_vma=False
    )
```

```python
import functools
import math

import jax
import jax.numpy as jnp
from jax import lax
from jax.experimental import pallas as pl
from jax.experimental.pallas import tpu as pltpu
from jax.sharding import PartitionSpec as P

UNROLL = 32
PIECES = 2


def _pack_kernel(slot_ref, *refs):
    x_refs, o_ref, buf = refs[:-2], refs[-2], refs[-1]
    buf[...] = jnp.zeros_like(buf)
    offset = 0
    for x_ref in x_refs:
        def body(j, carry, x_ref=x_ref, offset=offset):
            base = pl.multiple_of(j * UNROLL, UNROLL)
            for u in range(UNROLL):
                buf[pl.ds(slot_ref[offset + base + u], 1), :] = x_ref[pl.ds(base + u, 1), :]
            return carry

        lax.fori_loop(0, x_ref.shape[0] // UNROLL, body, 0)
        offset += x_ref.shape[0]
    width = buf.shape[1]
    n, lanes = o_ref.shape
    per = lanes // width
    lane = lax.broadcasted_iota(jnp.int32, (n, lanes), 1) // width
    acc = jnp.zeros((n, lanes), jnp.float32)
    for t in range(per):
        piece = buf[pl.ds(t, n, stride=per), :]
        wide = jnp.concatenate([piece] + [jnp.zeros_like(piece)] * (per - 1), axis=1)
        if t:
            wide = pltpu.roll(wide, shift=width * t, axis=1)
        acc = jnp.where(lane == t, wide, acc)
    o_ref[...] = acc


def _unpack_kernel(first, count, src_ref, *refs):
    v_refs, inc_ref, o_ref, joined, picked = refs[:-4], refs[-4], refs[-3], refs[-2], refs[-1]
    rows = sum(v_ref.shape[0] for v_ref in v_refs)
    width = v_refs[0].shape[1]
    n, lanes = inc_ref.shape
    per = lanes // width
    offset = 0
    for v_ref in v_refs:
        joined[pl.ds(offset, v_ref.shape[0]), :] = v_ref[...]
        offset += v_ref.shape[0]
    inc = inc_ref[...]
    for t in range(per):
        part = inc if t == 0 else pltpu.roll(inc, shift=lanes - width * t, axis=1)
        joined[pl.ds(rows + t, n, stride=per), :] = part[:, :width]

    def body(j, carry):
        base = pl.multiple_of(j * UNROLL, UNROLL)
        for u in range(UNROLL):
            picked[pl.ds(base + u, 1), :] = joined[pl.ds(src_ref[first + base + u], 1), :]
        return carry

    lax.fori_loop(0, count // UNROLL, body, 0)
    offset = 0
    for v_ref in v_refs:
        low = max(offset, first)
        high = min(offset + v_ref.shape[0], first + count)
        if low < high:
            o_ref[pl.ds(low - first, high - low), :] = (
                v_ref[pl.ds(low - offset, high - low), :] - picked[pl.ds(low - first, high - low), :]
            )
        offset += v_ref.shape[0]


def pack_rows(xs, send_pos):
    rows = sum(x.shape[0] for x in xs)
    width = xs[0].shape[1]
    return pl.pallas_call(
        _pack_kernel,
        in_specs=[pl.BlockSpec(memory_space=pltpu.SMEM)]
        + [pl.BlockSpec(memory_space=pltpu.VMEM)] * len(xs),
        out_specs=pl.BlockSpec(memory_space=pltpu.VMEM),
        out_shape=jax.ShapeDtypeStruct((rows * width // 128, 128), xs[0].dtype),
        scratch_shapes=[pltpu.VMEM((rows + 8, width), xs[0].dtype)],
        compiler_params=pltpu.CompilerParams(vmem_limit_bytes=48 * 1024 * 1024),
    )(send_pos, *xs)


def unpack_jump(vs, incoming, source, first, count):
    rows = sum(v.shape[0] for v in vs)
    width = vs[0].shape[1]
    return pl.pallas_call(
        functools.partial(_unpack_kernel, first, count),
        in_specs=[pl.BlockSpec(memory_space=pltpu.SMEM)]
        + [pl.BlockSpec(memory_space=pltpu.VMEM)] * (len(vs) + 1),
        out_specs=pl.BlockSpec(memory_space=pltpu.VMEM),
        out_shape=jax.ShapeDtypeStruct((count, width), vs[0].dtype),
        scratch_shapes=[
            pltpu.VMEM((2 * rows, width), vs[0].dtype),
            pltpu.VMEM((count, width), vs[0].dtype),
        ],
        compiler_params=pltpu.CompilerParams(vmem_limit_bytes=48 * 1024 * 1024),
    )(source, *vs, incoming)


def exchange(parts, send_pos):
    outgoing = pack_rows(parts, send_pos)
    return lax.all_to_all(outgoing, ("iface", "sub"), split_axis=0, concat_axis=0, tiled=True)


def apply_blocks(jump_rows, schur_blocks, sub_local, group):
    width = jump_rows.shape[1]
    half = jump_rows.astype(jnp.bfloat16).reshape(sub_local, group, width).transpose(2, 0, 1)
    ring = lax.axis_size("iface")
    here = lax.axis_index("iface")
    total = None
    for shift in range(ring):
        if shift:
            block = lax.ppermute(half, "iface", [(i, (i + shift) % ring) for i in range(ring)])
        else:
            block = half
        owner = (here - shift) % ring
        columns = lax.dynamic_slice_in_dim(schur_blocks, owner * group, group, axis=2)
        part = jnp.einsum("src,ksc->srk", columns, block, preferred_element_type=jnp.float32)
        total = part if total is None else total + part
    return total.reshape(sub_local * group, width)


def combine_weights(gram_matrix, picked, total_rows, sample_count):
    lower = jnp.linalg.cholesky(gram_matrix)
    solved = jax.scipy.linalg.cho_solve((lower, True), picked)
    coupling = jnp.dot(picked.T, solved, precision=lax.Precision.HIGHEST) * (
        total_rows / sample_count
    ) + jnp.eye(sample_count, dtype=jnp.float32)
    lower_two = jnp.linalg.cholesky(coupling)
    return jax.scipy.linalg.cho_solve((lower_two, True), solved.T) * (
        total_rows / math.sqrt(sample_count)
    )


def shards(schur_blocks, noise_field, peer_device, partner_slot, pivot_rows):
    sample_count, sub_local, group = noise_field.shape
    row_count = sub_local * group
    iface_count = lax.axis_size("iface")
    sub_count = lax.axis_size("sub")
    device_count = iface_count * sub_count
    capacity = row_count // device_count
    full_width = group * iface_count
    iface_place = lax.axis_index("iface")
    sub_place = lax.axis_index("sub")
    device_self = iface_place * sub_count + sub_place
    peer_flat = peer_device.reshape(row_count)
    slot_flat = partner_slot.reshape(row_count)
    crossing = peer_flat != device_self
    send_pos = jnp.clip(
        jnp.where(crossing, peer_flat * capacity + slot_flat, row_count), 0, row_count
    ).astype(jnp.int32)
    source = jnp.clip(
        jnp.where(crossing, row_count + peer_flat * capacity + slot_flat, slot_flat),
        0,
        2 * row_count - 1,
    ).astype(jnp.int32)
    routing = (send_pos, source)
    noise_rows = noise_field.transpose(1, 2, 0).reshape(row_count, sample_count)
    field = [noise_rows]
    step = row_count // PIECES
    sub_step = sub_local // PIECES
    for _ in range(2):
        incoming = exchange(field, send_pos)
        next_field = []
        for h in range(PIECES):
            jumped = unpack_jump(field, incoming, source, h * step, step)
            blocks = schur_blocks[h * sub_step:(h + 1) * sub_step]
            next_field.append(apply_blocks(jumped, blocks, sub_step, group))
        field = next_field
    incoming = exchange(field, send_pos)
    samples = unpack_jump(field, incoming, source, 0, row_count)
    gram_part = lax.dot_general(
        samples,
        samples,
        (((0,), (0,)), ((), ())),
        precision=lax.Precision.HIGHEST,
        preferred_element_type=jnp.float32,
    )
    pivot_sub = pivot_rows // full_width
    pivot_dof = pivot_rows % full_width
    holder = (pivot_sub // sub_local == sub_place) & (pivot_dof // group == iface_place)
    local_row = pivot_sub % sub_local * group + pivot_dof % group
    picked_part = jnp.take(samples, local_row, axis=0, mode="clip").T * holder[None, :].astype(
        jnp.float32
    )
    partial = jnp.concatenate((gram_part, picked_part), axis=1)[None]
    over_sub = jnp.sum(lax.all_gather(partial, "sub", axis=0, tiled=True), axis=0, keepdims=True)
    total = jnp.sum(lax.all_gather(over_sub, "iface", axis=0, tiled=True), axis=0)
    gram_matrix = total[:, :sample_count]
    picked = total[:, sample_count:]
    total_rows = float(sub_local * sub_count * full_width)
    coefficients = combine_weights(gram_matrix, picked, total_rows, sample_count)
    constraint_rows = lax.dot_general(
        coefficients,
        samples,
        (((1,), (1,)), ((), ())),
        precision=lax.Precision.HIGHEST,
        preferred_element_type=jnp.float32,
    )
    return constraint_rows.reshape(sample_count, sub_local, group)


def solution(mesh):
    placed = (
        P("sub", "iface", None),
        P(None, "sub", "iface"),
        P("sub", "iface"),
        P("sub", "iface"),
        P(),
    )
    return jax.shard_map(
        shards, mesh=mesh, in_specs=placed, out_specs=P(None, "sub", "iface"), check_vma=False
    )
```

```python
import functools
import math

import jax
import jax.numpy as jnp
from jax import lax
from jax.experimental import pallas as pl
from jax.experimental.pallas import tpu as pltpu
from jax.sharding import PartitionSpec as P

UNROLL = 64


def _pack_kernel(slot_ref, *refs):
    x_refs, o_ref, buf = refs[:-2], refs[-2], refs[-1]
    buf[...] = jnp.zeros_like(buf)
    offset = 0
    for x_ref in x_refs:
        def body(j, carry, x_ref=x_ref, offset=offset):
            base = pl.multiple_of(j * UNROLL, UNROLL)
            for u in range(UNROLL):
                buf[pl.ds(slot_ref[offset + base + u], 1), :] = x_ref[pl.ds(base + u, 1), :]
            return carry

        lax.fori_loop(0, x_ref.shape[0] // UNROLL, body, 0)
        offset += x_ref.shape[0]
    width = buf.shape[1]
    n, lanes = o_ref.shape
    per = lanes // width
    lane = lax.broadcasted_iota(jnp.int32, (n, lanes), 1) // width
    acc = jnp.zeros((n, lanes), jnp.float32)
    for t in range(per):
        piece = buf[pl.ds(t, n, stride=per), :]
        wide = jnp.concatenate([piece] + [jnp.zeros_like(piece)] * (per - 1), axis=1)
        if t:
            wide = pltpu.roll(wide, shift=width * t, axis=1)
        acc = jnp.where(lane == t, wide, acc)
    o_ref[...] = acc


def _unpack_kernel(first, count, src_ref, *refs):
    v_refs, inc_ref, o_ref, joined, picked = refs[:-4], refs[-4], refs[-3], refs[-2], refs[-1]
    rows = sum(v_ref.shape[0] for v_ref in v_refs)
    width = v_refs[0].shape[1]
    n, lanes = inc_ref.shape
    per = lanes // width
    offset = 0
    for v_ref in v_refs:
        joined[pl.ds(offset, v_ref.shape[0]), :] = v_ref[...]
        offset += v_ref.shape[0]
    inc = inc_ref[...]
    for t in range(per):
        part = inc if t == 0 else pltpu.roll(inc, shift=lanes - width * t, axis=1)
        joined[pl.ds(rows + t, n, stride=per), :] = part[:, :width]

    def body(j, carry):
        base = pl.multiple_of(j * UNROLL, UNROLL)
        for u in range(UNROLL):
            picked[pl.ds(base + u, 1), :] = joined[pl.ds(src_ref[first + base + u], 1), :]
        return carry

    lax.fori_loop(0, count // UNROLL, body, 0)
    offset = 0
    for v_ref in v_refs:
        low = max(offset, first)
        high = min(offset + v_ref.shape[0], first + count)
        if low < high:
            o_ref[pl.ds(low - first, high - low), :] = (
                v_ref[pl.ds(low - offset, high - low), :] - picked[pl.ds(low - first, high - low), :]
            )
        offset += v_ref.shape[0]


def pack_rows(xs, send_pos):
    rows = sum(x.shape[0] for x in xs)
    width = xs[0].shape[1]
    return pl.pallas_call(
        _pack_kernel,
        in_specs=[pl.BlockSpec(memory_space=pltpu.SMEM)]
        + [pl.BlockSpec(memory_space=pltpu.VMEM)] * len(xs),
        out_specs=pl.BlockSpec(memory_space=pltpu.VMEM),
        out_shape=jax.ShapeDtypeStruct((rows * width // 128, 128), xs[0].dtype),
        scratch_shapes=[pltpu.VMEM((rows + 8, width), xs[0].dtype)],
        compiler_params=pltpu.CompilerParams(vmem_limit_bytes=48 * 1024 * 1024),
    )(send_pos, *xs)


def unpack_jump(vs, incoming, source, first, count):
    rows = sum(v.shape[0] for v in vs)
    width = vs[0].shape[1]
    return pl.pallas_call(
        functools.partial(_unpack_kernel, first, count),
        in_specs=[pl.BlockSpec(memory_space=pltpu.SMEM)]
        + [pl.BlockSpec(memory_space=pltpu.VMEM)] * (len(vs) + 1),
        out_specs=pl.BlockSpec(memory_space=pltpu.VMEM),
        out_shape=jax.ShapeDtypeStruct((count, width), vs[0].dtype),
        scratch_shapes=[
            pltpu.VMEM((2 * rows, width), vs[0].dtype),
            pltpu.VMEM((count, width), vs[0].dtype),
        ],
        compiler_params=pltpu.CompilerParams(vmem_limit_bytes=48 * 1024 * 1024),
    )(source, *vs, incoming)


def exchange(parts, send_pos):
    outgoing = pack_rows(parts, send_pos)
    return lax.all_to_all(outgoing, ("iface", "sub"), split_axis=0, concat_axis=0, tiled=True)


def apply_blocks(jump_rows, schur_blocks, sub_local, group):
    width = jump_rows.shape[1]
    half = jump_rows.astype(jnp.bfloat16).reshape(sub_local, group, width).transpose(2, 0, 1)
    ring = lax.axis_size("iface")
    here = lax.axis_index("iface")
    total = None
    for shift in range(ring):
        if shift:
            block = lax.ppermute(half, "iface", [(i, (i + shift) % ring) for i in range(ring)])
        else:
            block = half
        owner = (here - shift) % ring
        columns = lax.dynamic_slice_in_dim(schur_blocks, owner * group, group, axis=2)
        part = jnp.einsum("src,ksc->srk", columns, block, preferred_element_type=jnp.float32)
        total = part if total is None else total + part
    return total.reshape(sub_local * group, width)


def combine_weights(gram_matrix, picked, total_rows, sample_count):
    lower = jnp.linalg.cholesky(gram_matrix)
    solved = jax.scipy.linalg.cho_solve((lower, True), picked)
    coupling = jnp.dot(picked.T, solved, precision=lax.Precision.HIGHEST) * (
        total_rows / sample_count
    ) + jnp.eye(sample_count, dtype=jnp.float32)
    lower_two = jnp.linalg.cholesky(coupling)
    return jax.scipy.linalg.cho_solve((lower_two, True), solved.T) * (
        total_rows / math.sqrt(sample_count)
    )


def shards(schur_blocks, noise_field, peer_device, partner_slot, pivot_rows):
    sample_count, sub_local, group = noise_field.shape
    row_count = sub_local * group
    iface_count = lax.axis_size("iface")
    sub_count = lax.axis_size("sub")
    device_count = iface_count * sub_count
    capacity = row_count // device_count
    full_width = group * iface_count
    iface_place = lax.axis_index("iface")
    sub_place = lax.axis_index("sub")
    device_self = iface_place * sub_count + sub_place
    peer_flat = peer_device.reshape(row_count)
    slot_flat = partner_slot.reshape(row_count)
    crossing = peer_flat != device_self
    send_pos = jnp.clip(
        jnp.where(crossing, peer_flat * capacity + slot_flat, row_count), 0, row_count
    ).astype(jnp.int32)
    source = jnp.clip(
        jnp.where(crossing, row_count + peer_flat * capacity + slot_flat, slot_flat),
        0,
        2 * row_count - 1,
    ).astype(jnp.int32)
    routing = (send_pos, source)
    noise_rows = noise_field.transpose(1, 2, 0).reshape(row_count, sample_count)
    field = [noise_rows]
    for _ in range(2):
        incoming = exchange(field, send_pos)
        jumped = unpack_jump(field, incoming, source, 0, row_count)
        field = [apply_blocks(jumped, schur_blocks, sub_local, group)]
    incoming = exchange(field, send_pos)
    samples = unpack_jump(field, incoming, source, 0, row_count)
    gram_part = lax.dot_general(
        samples,
        samples,
        (((0,), (0,)), ((), ())),
        precision=lax.Precision.HIGHEST,
        preferred_element_type=jnp.float32,
    )
    pivot_sub = pivot_rows // full_width
    pivot_dof = pivot_rows % full_width
    holder = (pivot_sub // sub_local == sub_place) & (pivot_dof // group == iface_place)
    local_row = pivot_sub % sub_local * group + pivot_dof % group
    picked_part = jnp.take(samples, local_row, axis=0, mode="clip").T * holder[None, :].astype(
        jnp.float32
    )
    partial = jnp.concatenate((gram_part, picked_part), axis=1)[None]
    over_sub = jnp.sum(lax.all_gather(partial, "sub", axis=0, tiled=True), axis=0)
    arrived = [over_sub] + [
        lax.ppermute(over_sub, "iface", [(i, (i + shift) % iface_count) for i in range(iface_count)])
        for shift in range(1, iface_count)
    ]
    stacked = jnp.stack(arrived)
    total = None
    for owner in range(iface_count):
        term = stacked[(iface_place - owner) % iface_count]
        total = term if total is None else total + term
    gram_matrix = total[:, :sample_count]
    picked = total[:, sample_count:]
    total_rows = float(sub_local * sub_count * full_width)
    coefficients = combine_weights(gram_matrix, picked, total_rows, sample_count)
    constraint_rows = lax.dot_general(
        coefficients,
        samples,
        (((1,), (1,)), ((), ())),
        precision=lax.Precision.HIGHEST,
        preferred_element_type=jnp.float32,
    )
    return constraint_rows.reshape(sample_count, sub_local, group)


def solution(mesh):
    placed = (
        P("sub", "iface", None),
        P(None, "sub", "iface"),
        P("sub", "iface"),
        P("sub", "iface"),
        P(),
    )
    return jax.shard_map(
        shards, mesh=mesh, in_specs=placed, out_specs=P(None, "sub", "iface"), check_vma=False
    )
```

```python
import functools
import math

import jax
import jax.numpy as jnp
from jax import lax
from jax.experimental import pallas as pl
from jax.experimental.pallas import tpu as pltpu
from jax.sharding import PartitionSpec as P

UNROLL = 64


def _pack_kernel(slot_ref, *refs):
    x_refs, o_ref, buf = refs[:-2], refs[-2], refs[-1]
    buf[...] = jnp.zeros_like(buf)
    offset = 0
    for x_ref in x_refs:
        def body(j, carry, x_ref=x_ref, offset=offset):
            base = pl.multiple_of(j * UNROLL, UNROLL)
            for u in range(UNROLL):
                buf[pl.ds(slot_ref[offset + base + u], 1), :] = x_ref[pl.ds(base + u, 1), :]
            return carry

        lax.fori_loop(0, x_ref.shape[0] // UNROLL, body, 0)
        offset += x_ref.shape[0]
    width = buf.shape[1]
    n, lanes = o_ref.shape
    per = lanes // width
    lane = lax.broadcasted_iota(jnp.int32, (n, lanes), 1) // width
    acc = jnp.zeros((n, lanes), jnp.float32)
    for t in range(per):
        piece = buf[pl.ds(t, n, stride=per), :]
        wide = jnp.concatenate([piece] + [jnp.zeros_like(piece)] * (per - 1), axis=1)
        if t:
            wide = pltpu.roll(wide, shift=width * t, axis=1)
        acc = jnp.where(lane == t, wide, acc)
    o_ref[...] = acc


def _unpack_kernel(first, count, src_ref, *refs):
    v_refs, inc_ref, o_ref, joined, picked = refs[:-4], refs[-4], refs[-3], refs[-2], refs[-1]
    rows = sum(v_ref.shape[0] for v_ref in v_refs)
    width = v_refs[0].shape[1]
    n, lanes = inc_ref.shape
    per = lanes // width
    offset = 0
    for v_ref in v_refs:
        joined[pl.ds(offset, v_ref.shape[0]), :] = v_ref[...]
        offset += v_ref.shape[0]
    inc = inc_ref[...]
    for t in range(per):
        part = inc if t == 0 else pltpu.roll(inc, shift=lanes - width * t, axis=1)
        joined[pl.ds(rows + t, n, stride=per), :] = part[:, :width]

    def body(j, carry):
        base = pl.multiple_of(j * UNROLL, UNROLL)
        for u in range(UNROLL):
            picked[pl.ds(base + u, 1), :] = joined[pl.ds(src_ref[first + base + u], 1), :]
        return carry

    lax.fori_loop(0, count // UNROLL, body, 0)
    offset = 0
    for v_ref in v_refs:
        low = max(offset, first)
        high = min(offset + v_ref.shape[0], first + count)
        if low < high:
            o_ref[pl.ds(low - first, high - low), :] = (
                v_ref[pl.ds(low - offset, high - low), :] - picked[pl.ds(low - first, high - low), :]
            )
        offset += v_ref.shape[0]


def pack_rows(xs, send_pos):
    rows = sum(x.shape[0] for x in xs)
    width = xs[0].shape[1]
    return pl.pallas_call(
        _pack_kernel,
        in_specs=[pl.BlockSpec(memory_space=pltpu.SMEM)]
        + [pl.BlockSpec(memory_space=pltpu.VMEM)] * len(xs),
        out_specs=pl.BlockSpec(memory_space=pltpu.VMEM),
        out_shape=jax.ShapeDtypeStruct((rows * width // 128, 128), xs[0].dtype),
        scratch_shapes=[pltpu.VMEM((rows + 8, width), xs[0].dtype)],
        compiler_params=pltpu.CompilerParams(vmem_limit_bytes=48 * 1024 * 1024),
    )(send_pos, *xs)


def unpack_jump(vs, incoming, source, first, count):
    rows = sum(v.shape[0] for v in vs)
    width = vs[0].shape[1]
    return pl.pallas_call(
        functools.partial(_unpack_kernel, first, count),
        in_specs=[pl.BlockSpec(memory_space=pltpu.SMEM)]
        + [pl.BlockSpec(memory_space=pltpu.VMEM)] * (len(vs) + 1),
        out_specs=pl.BlockSpec(memory_space=pltpu.VMEM),
        out_shape=jax.ShapeDtypeStruct((count, width), vs[0].dtype),
        scratch_shapes=[
            pltpu.VMEM((2 * rows, width), vs[0].dtype),
            pltpu.VMEM((count, width), vs[0].dtype),
        ],
        compiler_params=pltpu.CompilerParams(vmem_limit_bytes=48 * 1024 * 1024),
    )(source, *vs, incoming)


def exchange(parts, send_pos):
    outgoing = pack_rows(parts, send_pos)
    return lax.all_to_all(outgoing, ("iface", "sub"), split_axis=0, concat_axis=0, tiled=True)


def apply_blocks(jump_rows, schur_blocks, sub_local, group):
    width = jump_rows.shape[1]
    half = jump_rows.astype(jnp.bfloat16).reshape(sub_local, group, width).transpose(2, 0, 1)
    ring = lax.axis_size("iface")
    here = lax.axis_index("iface")
    total = None
    for shift in range(ring):
        if shift:
            block = lax.ppermute(half, "iface", [(i, (i + shift) % ring) for i in range(ring)])
        else:
            block = half
        owner = (here - shift) % ring
        columns = lax.dynamic_slice_in_dim(schur_blocks, owner * group, group, axis=2)
        part = jnp.einsum("src,ksc->srk", columns, block, preferred_element_type=jnp.float32)
        total = part if total is None else total + part
    return total.reshape(sub_local * group, width)


def combine_weights(gram_matrix, picked, total_rows, sample_count):
    lower = jnp.linalg.cholesky(gram_matrix)
    solved = jax.scipy.linalg.cho_solve((lower, True), picked)
    coupling = jnp.dot(picked.T, solved, precision=lax.Precision.HIGHEST) * (
        total_rows / sample_count
    ) + jnp.eye(sample_count, dtype=jnp.float32)
    lower_two = jnp.linalg.cholesky(coupling)
    return jax.scipy.linalg.cho_solve((lower_two, True), solved.T) * (
        total_rows / math.sqrt(sample_count)
    )


def shards(schur_blocks, noise_field, peer_device, partner_slot, pivot_rows):
    sample_count, sub_local, group = noise_field.shape
    row_count = sub_local * group
    iface_count = lax.axis_size("iface")
    sub_count = lax.axis_size("sub")
    device_count = iface_count * sub_count
    capacity = row_count // device_count
    full_width = group * iface_count
    iface_place = lax.axis_index("iface")
    sub_place = lax.axis_index("sub")
    device_self = iface_place * sub_count + sub_place
    peer_flat = peer_device.reshape(row_count)
    slot_flat = partner_slot.reshape(row_count)
    crossing = peer_flat != device_self
    send_pos = jnp.clip(
        jnp.where(crossing, peer_flat * capacity + slot_flat, row_count), 0, row_count
    ).astype(jnp.int32)
    source = jnp.clip(
        jnp.where(crossing, row_count + peer_flat * capacity + slot_flat, slot_flat),
        0,
        2 * row_count - 1,
    ).astype(jnp.int32)
    routing = (send_pos, source)
    noise_rows = noise_field.transpose(1, 2, 0).reshape(row_count, sample_count)
    field = [noise_rows]
    for _ in range(2):
        incoming = exchange(field, send_pos)
        jumped = unpack_jump(field, incoming, source, 0, row_count)
        field = [apply_blocks(jumped, schur_blocks, sub_local, group)]
    incoming = exchange(field, send_pos)
    samples = unpack_jump(field, incoming, source, 0, row_count)
    gram_part = lax.dot_general(
        samples,
        samples,
        (((0,), (0,)), ((), ())),
        precision=lax.Precision.HIGHEST,
        preferred_element_type=jnp.float32,
    )
    pivot_sub = pivot_rows // full_width
    pivot_dof = pivot_rows % full_width
    holder = (pivot_sub // sub_local == sub_place) & (pivot_dof // group == iface_place)
    local_row = pivot_sub % sub_local * group + pivot_dof % group
    picked_part = jnp.take(samples, local_row, axis=0, mode="clip").T * holder[None, :].astype(
        jnp.float32
    )
    partial = jnp.concatenate((gram_part, picked_part), axis=1)[None]
    over_sub = partial[0]
    span = 1
    while span < sub_count:
        over_sub = over_sub + lax.ppermute(
            over_sub, "sub", [(i, i ^ span) for i in range(sub_count)]
        )
        span *= 2
    arrived = [over_sub] + [
        lax.ppermute(over_sub, "iface", [(i, (i + shift) % iface_count) for i in range(iface_count)])
        for shift in range(1, iface_count)
    ]
    stacked = jnp.stack(arrived)
    total = None
    for owner in range(iface_count):
        term = stacked[(iface_place - owner) % iface_count]
        total = term if total is None else total + term
    gram_matrix = total[:, :sample_count]
    picked = total[:, sample_count:]
    total_rows = float(sub_local * sub_count * full_width)
    coefficients = combine_weights(gram_matrix, picked, total_rows, sample_count)
    constraint_rows = lax.dot_general(
        coefficients,
        samples,
        (((1,), (1,)), ((), ())),
        precision=lax.Precision.HIGHEST,
        preferred_element_type=jnp.float32,
    )
    return constraint_rows.reshape(sample_count, sub_local, group)


def solution(mesh):
    placed = (
        P("sub", "iface", None),
        P(None, "sub", "iface"),
        P("sub", "iface"),
        P("sub", "iface"),
        P(),
    )
    return jax.shard_map(
        shards, mesh=mesh, in_specs=placed, out_specs=P(None, "sub", "iface"), check_vma=False
    )
```

```python
import functools
import math

import jax
import jax.numpy as jnp
from jax import lax
from jax.experimental import pallas as pl
from jax.experimental.pallas import tpu as pltpu
from jax.sharding import PartitionSpec as P

UNROLL = 64


def _pack_kernel(slot_ref, *refs):
    x_refs, o_ref, buf = refs[:-2], refs[-2], refs[-1]
    buf[...] = jnp.zeros_like(buf)
    offset = 0
    for x_ref in x_refs:
        def body(j, carry, x_ref=x_ref, offset=offset):
            base = pl.multiple_of(j * UNROLL, UNROLL)
            for u in range(UNROLL):
                buf[pl.ds(slot_ref[offset + base + u], 1), :] = x_ref[pl.ds(base + u, 1), :]
            return carry

        lax.fori_loop(0, x_ref.shape[0] // UNROLL, body, 0)
        offset += x_ref.shape[0]
    width = buf.shape[1]
    n, lanes = o_ref.shape
    per = lanes // width
    lane = lax.broadcasted_iota(jnp.int32, (n, lanes), 1) // width
    acc = jnp.zeros((n, lanes), jnp.float32)
    for t in range(per):
        piece = buf[pl.ds(t, n, stride=per), :]
        wide = jnp.concatenate([piece] + [jnp.zeros_like(piece)] * (per - 1), axis=1)
        if t:
            wide = pltpu.roll(wide, shift=width * t, axis=1)
        acc = jnp.where(lane == t, wide, acc)
    o_ref[...] = acc


def _unpack_kernel(first, count, src_ref, *refs):
    v_refs, inc_ref, o_ref, joined, picked = refs[:-4], refs[-4], refs[-3], refs[-2], refs[-1]
    rows = sum(v_ref.shape[0] for v_ref in v_refs)
    width = v_refs[0].shape[1]
    n, lanes = inc_ref.shape
    per = lanes // width
    offset = 0
    for v_ref in v_refs:
        joined[pl.ds(offset, v_ref.shape[0]), :] = v_ref[...]
        offset += v_ref.shape[0]
    inc = inc_ref[...]
    for t in range(per):
        part = inc if t == 0 else pltpu.roll(inc, shift=lanes - width * t, axis=1)
        joined[pl.ds(rows + t, n, stride=per), :] = part[:, :width]

    def body(j, carry):
        base = pl.multiple_of(j * UNROLL, UNROLL)
        for u in range(UNROLL):
            picked[pl.ds(base + u, 1), :] = joined[pl.ds(src_ref[first + base + u], 1), :]
        return carry

    lax.fori_loop(0, count // UNROLL, body, 0)
    offset = 0
    for v_ref in v_refs:
        low = max(offset, first)
        high = min(offset + v_ref.shape[0], first + count)
        if low < high:
            o_ref[pl.ds(low - first, high - low), :] = (
                v_ref[pl.ds(low - offset, high - low), :] - picked[pl.ds(low - first, high - low), :]
            )
        offset += v_ref.shape[0]


def pack_rows(xs, send_pos):
    rows = sum(x.shape[0] for x in xs)
    width = xs[0].shape[1]
    return pl.pallas_call(
        _pack_kernel,
        in_specs=[pl.BlockSpec(memory_space=pltpu.SMEM)]
        + [pl.BlockSpec(memory_space=pltpu.VMEM)] * len(xs),
        out_specs=pl.BlockSpec(memory_space=pltpu.VMEM),
        out_shape=jax.ShapeDtypeStruct((rows * width // 128, 128), xs[0].dtype),
        scratch_shapes=[pltpu.VMEM((rows + 8, width), xs[0].dtype)],
        compiler_params=pltpu.CompilerParams(vmem_limit_bytes=48 * 1024 * 1024),
    )(send_pos, *xs)


def unpack_jump(vs, incoming, source, first, count):
    rows = sum(v.shape[0] for v in vs)
    width = vs[0].shape[1]
    return pl.pallas_call(
        functools.partial(_unpack_kernel, first, count),
        in_specs=[pl.BlockSpec(memory_space=pltpu.SMEM)]
        + [pl.BlockSpec(memory_space=pltpu.VMEM)] * (len(vs) + 1),
        out_specs=pl.BlockSpec(memory_space=pltpu.VMEM),
        out_shape=jax.ShapeDtypeStruct((count, width), vs[0].dtype),
        scratch_shapes=[
            pltpu.VMEM((2 * rows, width), vs[0].dtype),
            pltpu.VMEM((count, width), vs[0].dtype),
        ],
        compiler_params=pltpu.CompilerParams(vmem_limit_bytes=48 * 1024 * 1024),
    )(source, *vs, incoming)


def exchange(parts, send_pos):
    outgoing = pack_rows(parts, send_pos)
    return lax.all_to_all(outgoing, ("iface", "sub"), split_axis=0, concat_axis=0, tiled=True)


def apply_blocks(jump_rows, schur_blocks, sub_local, group):
    width = jump_rows.shape[1]
    half = jump_rows.astype(jnp.bfloat16).reshape(sub_local, group, width).transpose(2, 0, 1)
    ring = lax.axis_size("iface")
    here = lax.axis_index("iface")
    total = None
    for shift in range(ring):
        if shift:
            block = lax.ppermute(half, "iface", [(i, (i + shift) % ring) for i in range(ring)])
        else:
            block = half
        owner = (here - shift) % ring
        columns = lax.dynamic_slice_in_dim(schur_blocks, owner * group, group, axis=2)
        part = jnp.einsum("src,ksc->srk", columns, block, preferred_element_type=jnp.float32)
        total = part if total is None else total + part
    return total.reshape(sub_local * group, width)


def combine_weights(gram_matrix, picked, total_rows, sample_count):
    lower = jnp.linalg.cholesky(gram_matrix)
    solved = jax.scipy.linalg.cho_solve((lower, True), picked)
    coupling = jnp.dot(picked.T, solved, precision=lax.Precision.HIGHEST) * (
        total_rows / sample_count
    ) + jnp.eye(sample_count, dtype=jnp.float32)
    lower_two = jnp.linalg.cholesky(coupling)
    return jax.scipy.linalg.cho_solve((lower_two, True), solved.T) * (
        total_rows / math.sqrt(sample_count)
    )


def group_sum(x, axis, size):
    place = lax.axis_index(axis)
    bit = 1
    while bit < size:
        radix = min(4, size // bit)
        got = [x] + [
            lax.ppermute(x, axis, [(i, i ^ (m * bit)) for i in range(size)])
            for m in range(1, radix)
        ]
        stacked = jnp.stack(got)
        digit = (place // bit) % radix
        total = None
        for j in range(radix):
            term = stacked[jnp.bitwise_xor(digit, j)]
            total = term if total is None else total + term
        x = total
        bit *= radix
    return x


def shards(schur_blocks, noise_field, peer_device, partner_slot, pivot_rows):
    sample_count, sub_local, group = noise_field.shape
    row_count = sub_local * group
    iface_count = lax.axis_size("iface")
    sub_count = lax.axis_size("sub")
    device_count = iface_count * sub_count
    capacity = row_count // device_count
    full_width = group * iface_count
    iface_place = lax.axis_index("iface")
    sub_place = lax.axis_index("sub")
    device_self = iface_place * sub_count + sub_place
    peer_flat = peer_device.reshape(row_count)
    slot_flat = partner_slot.reshape(row_count)
    crossing = peer_flat != device_self
    send_pos = jnp.clip(
        jnp.where(crossing, peer_flat * capacity + slot_flat, row_count), 0, row_count
    ).astype(jnp.int32)
    source = jnp.clip(
        jnp.where(crossing, row_count + peer_flat * capacity + slot_flat, slot_flat),
        0,
        2 * row_count - 1,
    ).astype(jnp.int32)
    routing = (send_pos, source)
    noise_rows = noise_field.transpose(1, 2, 0).reshape(row_count, sample_count)
    field = [noise_rows]
    for _ in range(2):
        incoming = exchange(field, send_pos)
        jumped = unpack_jump(field, incoming, source, 0, row_count)
        field = [apply_blocks(jumped, schur_blocks, sub_local, group)]
    incoming = exchange(field, send_pos)
    samples = unpack_jump(field, incoming, source, 0, row_count)
    gram_part = lax.dot_general(
        samples,
        samples,
        (((0,), (0,)), ((), ())),
        precision=lax.Precision.HIGHEST,
        preferred_element_type=jnp.float32,
    )
    pivot_sub = pivot_rows // full_width
    pivot_dof = pivot_rows % full_width
    holder = (pivot_sub // sub_local == sub_place) & (pivot_dof // group == iface_place)
    local_row = pivot_sub % sub_local * group + pivot_dof % group
    picked_part = jnp.take(samples, local_row, axis=0, mode="clip").T * holder[None, :].astype(
        jnp.float32
    )
    partial = jnp.concatenate((gram_part, picked_part), axis=1)[None]
    total = group_sum(group_sum(partial[0], "sub", sub_count), "iface", iface_count)
    gram_matrix = total[:, :sample_count]
    picked = total[:, sample_count:]
    total_rows = float(sub_local * sub_count * full_width)
    coefficients = combine_weights(gram_matrix, picked, total_rows, sample_count)
    constraint_rows = lax.dot_general(
        coefficients,
        samples,
        (((1,), (1,)), ((), ())),
        precision=lax.Precision.HIGHEST,
        preferred_element_type=jnp.float32,
    )
    return constraint_rows.reshape(sample_count, sub_local, group)


def solution(mesh):
    placed = (
        P("sub", "iface", None),
        P(None, "sub", "iface"),
        P("sub", "iface"),
        P("sub", "iface"),
        P(),
    )
    return jax.shard_map(
        shards, mesh=mesh, in_specs=placed, out_specs=P(None, "sub", "iface"), check_vma=False
    )
```

```python
import functools
import math

import jax
import jax.numpy as jnp
from jax import lax
from jax.experimental import pallas as pl
from jax.experimental.pallas import tpu as pltpu
from jax.sharding import PartitionSpec as P

UNROLL = 64


def _pack_kernel(slot_ref, *refs):
    x_refs, o_ref, buf = refs[:-2], refs[-2], refs[-1]
    buf[...] = jnp.zeros_like(buf)
    offset = 0
    for x_ref in x_refs:
        def body(j, carry, x_ref=x_ref, offset=offset):
            base = pl.multiple_of(j * UNROLL, UNROLL)
            for u in range(UNROLL):
                buf[pl.ds(slot_ref[offset + base + u], 1), :] = x_ref[pl.ds(base + u, 1), :]
            return carry

        lax.fori_loop(0, x_ref.shape[0] // UNROLL, body, 0)
        offset += x_ref.shape[0]
    width = buf.shape[1]
    n, lanes = o_ref.shape
    per = lanes // width
    lane = lax.broadcasted_iota(jnp.int32, (n, lanes), 1) // width
    acc = jnp.zeros((n, lanes), jnp.float32)
    for t in range(per):
        piece = buf[pl.ds(t, n, stride=per), :]
        wide = jnp.concatenate([piece] + [jnp.zeros_like(piece)] * (per - 1), axis=1)
        if t:
            wide = pltpu.roll(wide, shift=width * t, axis=1)
        acc = jnp.where(lane == t, wide, acc)
    o_ref[...] = acc


def _unpack_kernel(first, count, src_ref, *refs):
    v_refs, inc_ref, o_ref, joined, picked = refs[:-4], refs[-4], refs[-3], refs[-2], refs[-1]
    rows = sum(v_ref.shape[0] for v_ref in v_refs)
    width = v_refs[0].shape[1]
    n, lanes = inc_ref.shape
    per = lanes // width
    offset = 0
    for v_ref in v_refs:
        joined[pl.ds(offset, v_ref.shape[0]), :] = v_ref[...]
        offset += v_ref.shape[0]
    inc = inc_ref[...]
    for t in range(per):
        part = inc if t == 0 else pltpu.roll(inc, shift=lanes - width * t, axis=1)
        joined[pl.ds(rows + t, n, stride=per), :] = part[:, :width]

    def body(j, carry):
        base = pl.multiple_of(j * UNROLL, UNROLL)
        for u in range(UNROLL):
            picked[pl.ds(base + u, 1), :] = joined[pl.ds(src_ref[first + base + u], 1), :]
        return carry

    lax.fori_loop(0, count // UNROLL, body, 0)
    offset = 0
    for v_ref in v_refs:
        low = max(offset, first)
        high = min(offset + v_ref.shape[0], first + count)
        if low < high:
            o_ref[pl.ds(low - first, high - low), :] = (
                v_ref[pl.ds(low - offset, high - low), :] - picked[pl.ds(low - first, high - low), :]
            )
        offset += v_ref.shape[0]


def pack_rows(xs, send_pos):
    rows = sum(x.shape[0] for x in xs)
    width = xs[0].shape[1]
    return pl.pallas_call(
        _pack_kernel,
        in_specs=[pl.BlockSpec(memory_space=pltpu.SMEM)]
        + [pl.BlockSpec(memory_space=pltpu.VMEM)] * len(xs),
        out_specs=pl.BlockSpec(memory_space=pltpu.VMEM),
        out_shape=jax.ShapeDtypeStruct((rows * width // 128, 128), xs[0].dtype),
        scratch_shapes=[pltpu.VMEM((rows + 8, width), xs[0].dtype)],
        compiler_params=pltpu.CompilerParams(vmem_limit_bytes=48 * 1024 * 1024),
    )(send_pos, *xs)


def unpack_jump(vs, incoming, source, first, count):
    rows = sum(v.shape[0] for v in vs)
    width = vs[0].shape[1]
    return pl.pallas_call(
        functools.partial(_unpack_kernel, first, count),
        in_specs=[pl.BlockSpec(memory_space=pltpu.SMEM)]
        + [pl.BlockSpec(memory_space=pltpu.VMEM)] * (len(vs) + 1),
        out_specs=pl.BlockSpec(memory_space=pltpu.VMEM),
        out_shape=jax.ShapeDtypeStruct((count, width), vs[0].dtype),
        scratch_shapes=[
            pltpu.VMEM((2 * rows, width), vs[0].dtype),
            pltpu.VMEM((count, width), vs[0].dtype),
        ],
        compiler_params=pltpu.CompilerParams(vmem_limit_bytes=48 * 1024 * 1024),
    )(source, *vs, incoming)


def exchange(parts, send_pos):
    outgoing = pack_rows(parts, send_pos)
    return lax.all_to_all(outgoing, ("iface", "sub"), split_axis=0, concat_axis=0, tiled=True)


def apply_blocks(jump_rows, schur_blocks, sub_local, group):
    width = jump_rows.shape[1]
    half = jump_rows.astype(jnp.bfloat16).reshape(sub_local, group, width).transpose(2, 0, 1)
    ring = lax.axis_size("iface")
    here = lax.axis_index("iface")

    def shifted(value, shift):
        return lax.ppermute(value, "iface", [(i, (i + shift) % ring) for i in range(ring)])

    def product(block, owner):
        columns = lax.dynamic_slice_in_dim(schur_blocks, owner * group, group, axis=2)
        return jnp.einsum("src,ksc->srk", columns, block, preferred_element_type=jnp.float32)

    if ring == 4:
        from_left = shifted(half, 1)
        from_right = shifted(half, ring - 1)
        split = width // 2
        far = jnp.concatenate(
            (shifted(from_left[:split], 1), shifted(from_right[split:], ring - 1)), axis=0
        )
        total = product(half, here)
        total = total + product(from_left, (here + ring - 1) % ring)
        total = total + product(from_right, (here + 1) % ring)
        total = total + product(far, (here + 2) % ring)
    else:
        total = None
        for shift in range(ring):
            block = shifted(half, shift) if shift else half
            part = product(block, (here - shift) % ring)
            total = part if total is None else total + part
    return total.reshape(sub_local * group, width)


def combine_weights(gram_matrix, picked, total_rows, sample_count):
    lower = jnp.linalg.cholesky(gram_matrix)
    solved = jax.scipy.linalg.cho_solve((lower, True), picked)
    coupling = jnp.dot(picked.T, solved, precision=lax.Precision.HIGHEST) * (
        total_rows / sample_count
    ) + jnp.eye(sample_count, dtype=jnp.float32)
    lower_two = jnp.linalg.cholesky(coupling)
    return jax.scipy.linalg.cho_solve((lower_two, True), solved.T) * (
        total_rows / math.sqrt(sample_count)
    )


def group_sum(x, axis, size):
    place = lax.axis_index(axis)
    bit = 1
    while bit < size:
        radix = min(4, size // bit)
        got = [x] + [
            lax.ppermute(x, axis, [(i, i ^ (m * bit)) for i in range(size)])
            for m in range(1, radix)
        ]
        stacked = jnp.stack(got)
        digit = (place // bit) % radix
        total = None
        for j in range(radix):
            term = stacked[jnp.bitwise_xor(digit, j)]
            total = term if total is None else total + term
        x = total
        bit *= radix
    return x


def shards(schur_blocks, noise_field, peer_device, partner_slot, pivot_rows):
    sample_count, sub_local, group = noise_field.shape
    row_count = sub_local * group
    iface_count = lax.axis_size("iface")
    sub_count = lax.axis_size("sub")
    device_count = iface_count * sub_count
    capacity = row_count // device_count
    full_width = group * iface_count
    iface_place = lax.axis_index("iface")
    sub_place = lax.axis_index("sub")
    device_self = iface_place * sub_count + sub_place
    peer_flat = peer_device.reshape(row_count)
    slot_flat = partner_slot.reshape(row_count)
    crossing = peer_flat != device_self
    send_pos = jnp.clip(
        jnp.where(crossing, peer_flat * capacity + slot_flat, row_count), 0, row_count
    ).astype(jnp.int32)
    source = jnp.clip(
        jnp.where(crossing, row_count + peer_flat * capacity + slot_flat, slot_flat),
        0,
        2 * row_count - 1,
    ).astype(jnp.int32)
    routing = (send_pos, source)
    noise_rows = noise_field.transpose(1, 2, 0).reshape(row_count, sample_count)
    field = [noise_rows]
    for _ in range(2):
        incoming = exchange(field, send_pos)
        jumped = unpack_jump(field, incoming, source, 0, row_count)
        field = [apply_blocks(jumped, schur_blocks, sub_local, group)]
    incoming = exchange(field, send_pos)
    samples = unpack_jump(field, incoming, source, 0, row_count)
    gram_part = lax.dot_general(
        samples,
        samples,
        (((0,), (0,)), ((), ())),
        precision=lax.Precision.HIGHEST,
        preferred_element_type=jnp.float32,
    )
    pivot_sub = pivot_rows // full_width
    pivot_dof = pivot_rows % full_width
    holder = (pivot_sub // sub_local == sub_place) & (pivot_dof // group == iface_place)
    local_row = pivot_sub % sub_local * group + pivot_dof % group
    picked_part = jnp.take(samples, local_row, axis=0, mode="clip").T * holder[None, :].astype(
        jnp.float32
    )
    partial = jnp.concatenate((gram_part, picked_part), axis=1)[None]
    total = group_sum(group_sum(partial[0], "sub", sub_count), "iface", iface_count)
    gram_matrix = total[:, :sample_count]
    picked = total[:, sample_count:]
    total_rows = float(sub_local * sub_count * full_width)
    coefficients = combine_weights(gram_matrix, picked, total_rows, sample_count)
    constraint_rows = lax.dot_general(
        coefficients,
        samples,
        (((1,), (1,)), ((), ())),
        precision=lax.Precision.HIGHEST,
        preferred_element_type=jnp.float32,
    )
    return constraint_rows.reshape(sample_count, sub_local, group)


def solution(mesh):
    placed = (
        P("sub", "iface", None),
        P(None, "sub", "iface"),
        P("sub", "iface"),
        P("sub", "iface"),
        P(),
    )
    return jax.shard_map(
        shards, mesh=mesh, in_specs=placed, out_specs=P(None, "sub", "iface"), check_vma=False
    )
```

```python
import functools
import math

import jax
import jax.numpy as jnp
from jax import lax
from jax.experimental import pallas as pl
from jax.experimental.pallas import tpu as pltpu
from jax.sharding import PartitionSpec as P

UNROLL = 64


def _pack_kernel(slot_ref, *refs):
    x_refs, o_ref, buf = refs[:-2], refs[-2], refs[-1]
    buf[...] = jnp.zeros_like(buf)
    offset = 0
    for x_ref in x_refs:
        def body(j, carry, x_ref=x_ref, offset=offset):
            base = pl.multiple_of(j * UNROLL, UNROLL)
            for u in range(UNROLL):
                buf[pl.ds(slot_ref[offset + base + u], 1), :] = x_ref[pl.ds(base + u, 1), :]
            return carry

        lax.fori_loop(0, x_ref.shape[0] // UNROLL, body, 0)
        offset += x_ref.shape[0]
    width = buf.shape[1]
    n, lanes = o_ref.shape
    per = lanes // width
    lane = lax.broadcasted_iota(jnp.int32, (n, lanes), 1) // width
    acc = jnp.zeros((n, lanes), jnp.float32)
    for t in range(per):
        piece = buf[pl.ds(t, n, stride=per), :]
        wide = jnp.concatenate([piece] + [jnp.zeros_like(piece)] * (per - 1), axis=1)
        if t:
            wide = pltpu.roll(wide, shift=width * t, axis=1)
        acc = jnp.where(lane == t, wide, acc)
    o_ref[...] = acc


def _unpack_kernel(first, count, src_ref, *refs):
    v_refs, inc_ref, o_ref, joined, picked = refs[:-4], refs[-4], refs[-3], refs[-2], refs[-1]
    rows = sum(v_ref.shape[0] for v_ref in v_refs)
    width = v_refs[0].shape[1]
    n, lanes = inc_ref.shape
    per = lanes // width
    offset = 0
    for v_ref in v_refs:
        joined[pl.ds(offset, v_ref.shape[0]), :] = v_ref[...]
        offset += v_ref.shape[0]
    inc = inc_ref[...]
    for t in range(per):
        part = inc if t == 0 else pltpu.roll(inc, shift=lanes - width * t, axis=1)
        joined[pl.ds(rows + t, n, stride=per), :] = part[:, :width]

    def body(j, carry):
        base = pl.multiple_of(j * UNROLL, UNROLL)
        for u in range(UNROLL):
            picked[pl.ds(base + u, 1), :] = joined[pl.ds(src_ref[first + base + u], 1), :]
        return carry

    lax.fori_loop(0, count // UNROLL, body, 0)
    offset = 0
    for v_ref in v_refs:
        low = max(offset, first)
        high = min(offset + v_ref.shape[0], first + count)
        if low < high:
            o_ref[pl.ds(low - first, high - low), :] = (
                v_ref[pl.ds(low - offset, high - low), :] - picked[pl.ds(low - first, high - low), :]
            )
        offset += v_ref.shape[0]


def pack_rows(xs, send_pos):
    rows = sum(x.shape[0] for x in xs)
    width = xs[0].shape[1]
    return pl.pallas_call(
        _pack_kernel,
        in_specs=[pl.BlockSpec(memory_space=pltpu.SMEM)]
        + [pl.BlockSpec(memory_space=pltpu.VMEM)] * len(xs),
        out_specs=pl.BlockSpec(memory_space=pltpu.VMEM),
        out_shape=jax.ShapeDtypeStruct((rows * width // 128, 128), xs[0].dtype),
        scratch_shapes=[pltpu.VMEM((rows + 8, width), xs[0].dtype)],
        compiler_params=pltpu.CompilerParams(vmem_limit_bytes=48 * 1024 * 1024),
    )(send_pos, *xs)


def unpack_jump(vs, incoming, source, first, count):
    rows = sum(v.shape[0] for v in vs)
    width = vs[0].shape[1]
    return pl.pallas_call(
        functools.partial(_unpack_kernel, first, count),
        in_specs=[pl.BlockSpec(memory_space=pltpu.SMEM)]
        + [pl.BlockSpec(memory_space=pltpu.VMEM)] * (len(vs) + 1),
        out_specs=pl.BlockSpec(memory_space=pltpu.VMEM),
        out_shape=jax.ShapeDtypeStruct((count, width), vs[0].dtype),
        scratch_shapes=[
            pltpu.VMEM((2 * rows, width), vs[0].dtype),
            pltpu.VMEM((count, width), vs[0].dtype),
        ],
        compiler_params=pltpu.CompilerParams(vmem_limit_bytes=48 * 1024 * 1024),
    )(source, *vs, incoming)


def exchange(parts, send_pos):
    outgoing = pack_rows(parts, send_pos)
    return lax.all_to_all(outgoing, ("iface", "sub"), split_axis=0, concat_axis=0, tiled=True)


def apply_blocks(jump_rows, schur_blocks, sub_local, group):
    width = jump_rows.shape[1]
    half = jump_rows.astype(jnp.bfloat16).reshape(sub_local, group, width).transpose(2, 0, 1)
    ring = lax.axis_size("iface")
    here = lax.axis_index("iface")

    def shifted(value, shift):
        return lax.ppermute(value, "iface", [(i, (i + shift) % ring) for i in range(ring)])

    def product(block, owner):
        columns = lax.dynamic_slice_in_dim(schur_blocks, owner * group, group, axis=2)
        return jnp.einsum("src,ksc->srk", columns, block, preferred_element_type=jnp.float32)

    if ring == 4:
        from_left = shifted(half, 1)
        from_right = shifted(half, ring - 1)
        split = width // 2
        far = jnp.concatenate(
            (shifted(from_left[:split], 1), shifted(from_right[split:], ring - 1)), axis=0
        )
        total = product(half, here)
        total = total + product(from_left, (here + ring - 1) % ring)
        total = total + product(from_right, (here + 1) % ring)
        total = total + product(far, (here + 2) % ring)
    else:
        total = None
        for shift in range(ring):
            block = shifted(half, shift) if shift else half
            part = product(block, (here - shift) % ring)
            total = part if total is None else total + part
    return total.reshape(sub_local * group, width)


def combine_weights(gram_matrix, picked, total_rows, sample_count):
    lower = jnp.linalg.cholesky(gram_matrix)
    solved = jax.scipy.linalg.cho_solve((lower, True), picked)
    coupling = jnp.dot(picked.T, solved, precision=lax.Precision.HIGHEST) * (
        total_rows / sample_count
    ) + jnp.eye(sample_count, dtype=jnp.float32)
    lower_two = jnp.linalg.cholesky(coupling)
    return jax.scipy.linalg.cho_solve((lower_two, True), solved.T) * (
        total_rows / math.sqrt(sample_count)
    )


def group_sum(x, axis, size):
    place = lax.axis_index(axis)
    bit = 1
    while bit < size:
        radix = min(4, size // bit)
        got = [x] + [
            lax.ppermute(x, axis, [(i, i ^ (m * bit)) for i in range(size)])
            for m in range(1, radix)
        ]
        stacked = jnp.stack(got)
        digit = (place // bit) % radix
        total = None
        for j in range(radix):
            term = stacked[jnp.bitwise_xor(digit, j)]
            total = term if total is None else total + term
        x = total
        bit *= radix
    return x


def shards(schur_blocks, noise_field, peer_device, partner_slot, pivot_rows):
    sample_count, sub_local, group = noise_field.shape
    row_count = sub_local * group
    iface_count = lax.axis_size("iface")
    sub_count = lax.axis_size("sub")
    device_count = iface_count * sub_count
    capacity = row_count // device_count
    full_width = group * iface_count
    iface_place = lax.axis_index("iface")
    sub_place = lax.axis_index("sub")
    device_self = iface_place * sub_count + sub_place
    peer_flat = peer_device.reshape(row_count)
    slot_flat = partner_slot.reshape(row_count)
    crossing = peer_flat != device_self
    send_pos = jnp.clip(
        jnp.where(crossing, peer_flat * capacity + slot_flat, row_count), 0, row_count
    ).astype(jnp.int32)
    source = jnp.clip(
        jnp.where(crossing, row_count + peer_flat * capacity + slot_flat, slot_flat),
        0,
        2 * row_count - 1,
    ).astype(jnp.int32)
    routing = (send_pos, source)
    noise_rows = noise_field.transpose(1, 2, 0).reshape(row_count, sample_count)
    field = [noise_rows]
    for _ in range(2):
        incoming = exchange(field, send_pos)
        jumped = unpack_jump(field, incoming, source, 0, row_count)
        field = [apply_blocks(jumped, schur_blocks, sub_local, group)]
    incoming = exchange(field, send_pos)
    samples = unpack_jump(field, incoming, source, 0, row_count)
    gram_part = lax.dot_general(
        samples,
        samples,
        (((0,), (0,)), ((), ())),
        precision=lax.Precision.HIGHEST,
        preferred_element_type=jnp.float32,
    )
    pivot_sub = pivot_rows // full_width
    pivot_dof = pivot_rows % full_width
    holder = (pivot_sub // sub_local == sub_place) & (pivot_dof // group == iface_place)
    local_row = pivot_sub % sub_local * group + pivot_dof % group
    picked_part = jnp.take(samples, local_row, axis=0, mode="clip").T * holder[None, :].astype(
        jnp.float32
    )
    partial = jnp.concatenate((gram_part, picked_part), axis=1)[None]
    total = group_sum(group_sum(partial[0], "sub", sub_count), "iface", iface_count)
    gram_matrix = total[:, :sample_count]
    picked = total[:, sample_count:]
    total_rows = float(sub_local * sub_count * full_width)
    coefficients = combine_weights(gram_matrix, picked, total_rows, sample_count)
    constraint_rows = lax.dot_general(
        coefficients,
        samples,
        (((1,), (1,)), ((), ())),
        precision=lax.Precision.HIGH,
        preferred_element_type=jnp.float32,
    )
    return constraint_rows.reshape(sample_count, sub_local, group)


def solution(mesh):
    placed = (
        P("sub", "iface", None),
        P(None, "sub", "iface"),
        P("sub", "iface"),
        P("sub", "iface"),
        P(),
    )
    return jax.shard_map(
        shards, mesh=mesh, in_specs=placed, out_specs=P(None, "sub", "iface"), check_vma=False
    )
```

```python
import functools
import math

import jax
import jax.numpy as jnp
from jax import lax
from jax.experimental import pallas as pl
from jax.experimental.pallas import tpu as pltpu
from jax.sharding import PartitionSpec as P

UNROLL = 128


def _pack_kernel(slot_ref, *refs):
    x_refs, o_ref, buf = refs[:-2], refs[-2], refs[-1]
    buf[...] = jnp.zeros_like(buf)
    offset = 0
    for x_ref in x_refs:
        def body(j, carry, x_ref=x_ref, offset=offset):
            base = pl.multiple_of(j * UNROLL, UNROLL)
            for u in range(UNROLL):
                buf[pl.ds(slot_ref[offset + base + u], 1), :] = x_ref[pl.ds(base + u, 1), :]
            return carry

        lax.fori_loop(0, x_ref.shape[0] // UNROLL, body, 0)
        offset += x_ref.shape[0]
    width = buf.shape[1]
    n, lanes = o_ref.shape
    per = lanes // width
    lane = lax.broadcasted_iota(jnp.int32, (n, lanes), 1) // width
    acc = jnp.zeros((n, lanes), jnp.float32)
    for t in range(per):
        piece = buf[pl.ds(t, n, stride=per), :]
        wide = jnp.concatenate([piece] + [jnp.zeros_like(piece)] * (per - 1), axis=1)
        if t:
            wide = pltpu.roll(wide, shift=width * t, axis=1)
        acc = jnp.where(lane == t, wide, acc)
    o_ref[...] = acc


def _unpack_kernel(first, count, src_ref, *refs):
    v_refs, inc_ref, o_ref, joined, picked = refs[:-4], refs[-4], refs[-3], refs[-2], refs[-1]
    rows = sum(v_ref.shape[0] for v_ref in v_refs)
    width = v_refs[0].shape[1]
    n, lanes = inc_ref.shape
    per = lanes // width
    offset = 0
    for v_ref in v_refs:
        joined[pl.ds(offset, v_ref.shape[0]), :] = v_ref[...]
        offset += v_ref.shape[0]
    inc = inc_ref[...]
    for t in range(per):
        part = inc if t == 0 else pltpu.roll(inc, shift=lanes - width * t, axis=1)
        joined[pl.ds(rows + t, n, stride=per), :] = part[:, :width]

    def body(j, carry):
        base = pl.multiple_of(j * UNROLL, UNROLL)
        for u in range(UNROLL):
            picked[pl.ds(base + u, 1), :] = joined[pl.ds(src_ref[first + base + u], 1), :]
        return carry

    lax.fori_loop(0, count // UNROLL, body, 0)
    offset = 0
    for v_ref in v_refs:
        low = max(offset, first)
        high = min(offset + v_ref.shape[0], first + count)
        if low < high:
            o_ref[pl.ds(low - first, high - low), :] = (
                v_ref[pl.ds(low - offset, high - low), :] - picked[pl.ds(low - first, high - low), :]
            )
        offset += v_ref.shape[0]


def pack_rows(xs, send_pos):
    rows = sum(x.shape[0] for x in xs)
    width = xs[0].shape[1]
    return pl.pallas_call(
        _pack_kernel,
        in_specs=[pl.BlockSpec(memory_space=pltpu.SMEM)]
        + [pl.BlockSpec(memory_space=pltpu.VMEM)] * len(xs),
        out_specs=pl.BlockSpec(memory_space=pltpu.VMEM),
        out_shape=jax.ShapeDtypeStruct((rows * width // 128, 128), xs[0].dtype),
        scratch_shapes=[pltpu.VMEM((rows + 8, width), xs[0].dtype)],
        compiler_params=pltpu.CompilerParams(vmem_limit_bytes=48 * 1024 * 1024),
    )(send_pos, *xs)


def unpack_jump(vs, incoming, source, first, count):
    rows = sum(v.shape[0] for v in vs)
    width = vs[0].shape[1]
    return pl.pallas_call(
        functools.partial(_unpack_kernel, first, count),
        in_specs=[pl.BlockSpec(memory_space=pltpu.SMEM)]
        + [pl.BlockSpec(memory_space=pltpu.VMEM)] * (len(vs) + 1),
        out_specs=pl.BlockSpec(memory_space=pltpu.VMEM),
        out_shape=jax.ShapeDtypeStruct((count, width), vs[0].dtype),
        scratch_shapes=[
            pltpu.VMEM((2 * rows, width), vs[0].dtype),
            pltpu.VMEM((count, width), vs[0].dtype),
        ],
        compiler_params=pltpu.CompilerParams(vmem_limit_bytes=48 * 1024 * 1024),
    )(source, *vs, incoming)


def exchange(parts, send_pos):
    outgoing = pack_rows(parts, send_pos)
    return lax.all_to_all(outgoing, ("iface", "sub"), split_axis=0, concat_axis=0, tiled=True)


def apply_blocks(jump_rows, schur_blocks, sub_local, group):
    width = jump_rows.shape[1]
    half = jump_rows.astype(jnp.bfloat16).reshape(sub_local, group, width).transpose(2, 0, 1)
    ring = lax.axis_size("iface")
    here = lax.axis_index("iface")

    def shifted(value, shift):
        return lax.ppermute(value, "iface", [(i, (i + shift) % ring) for i in range(ring)])

    def product(block, owner):
        columns = lax.dynamic_slice_in_dim(schur_blocks, owner * group, group, axis=2)
        return jnp.einsum("src,ksc->srk", columns, block, preferred_element_type=jnp.float32)

    if ring == 4:
        from_left = shifted(half, 1)
        from_right = shifted(half, ring - 1)
        split = width // 2
        far = jnp.concatenate(
            (shifted(from_left[:split], 1), shifted(from_right[split:], ring - 1)), axis=0
        )
        total = product(half, here)
        total = total + product(from_left, (here + ring - 1) % ring)
        total = total + product(from_right, (here + 1) % ring)
        total = total + product(far, (here + 2) % ring)
    else:
        total = None
        for shift in range(ring):
            block = shifted(half, shift) if shift else half
            part = product(block, (here - shift) % ring)
            total = part if total is None else total + part
    return total.reshape(sub_local * group, width)


def combine_weights(gram_matrix, picked, total_rows, sample_count):
    lower = jnp.linalg.cholesky(gram_matrix)
    solved = jax.scipy.linalg.cho_solve((lower, True), picked)
    coupling = jnp.dot(picked.T, solved, precision=lax.Precision.HIGHEST) * (
        total_rows / sample_count
    ) + jnp.eye(sample_count, dtype=jnp.float32)
    lower_two = jnp.linalg.cholesky(coupling)
    return jax.scipy.linalg.cho_solve((lower_two, True), solved.T) * (
        total_rows / math.sqrt(sample_count)
    )


def group_sum(x, axis, size):
    place = lax.axis_index(axis)
    bit = 1
    while bit < size:
        radix = min(4, size // bit)
        got = [x] + [
            lax.ppermute(x, axis, [(i, i ^ (m * bit)) for i in range(size)])
            for m in range(1, radix)
        ]
        stacked = jnp.stack(got)
        digit = (place // bit) % radix
        total = None
        for j in range(radix):
            term = stacked[jnp.bitwise_xor(digit, j)]
            total = term if total is None else total + term
        x = total
        bit *= radix
    return x


def shards(schur_blocks, noise_field, peer_device, partner_slot, pivot_rows):
    sample_count, sub_local, group = noise_field.shape
    row_count = sub_local * group
    iface_count = lax.axis_size("iface")
    sub_count = lax.axis_size("sub")
    device_count = iface_count * sub_count
    capacity = row_count // device_count
    full_width = group * iface_count
    iface_place = lax.axis_index("iface")
    sub_place = lax.axis_index("sub")
    device_self = iface_place * sub_count + sub_place
    peer_flat = peer_device.reshape(row_count)
    slot_flat = partner_slot.reshape(row_count)
    crossing = peer_flat != device_self
    send_pos = jnp.clip(
        jnp.where(crossing, peer_flat * capacity + slot_flat, row_count), 0, row_count
    ).astype(jnp.int32)
    source = jnp.clip(
        jnp.where(crossing, row_count + peer_flat * capacity + slot_flat, slot_flat),
        0,
        2 * row_count - 1,
    ).astype(jnp.int32)
    routing = (send_pos, source)
    noise_rows = noise_field.transpose(1, 2, 0).reshape(row_count, sample_count)
    field = [noise_rows]
    for _ in range(2):
        incoming = exchange(field, send_pos)
        jumped = unpack_jump(field, incoming, source, 0, row_count)
        field = [apply_blocks(jumped, schur_blocks, sub_local, group)]
    incoming = exchange(field, send_pos)
    samples = unpack_jump(field, incoming, source, 0, row_count)
    gram_part = lax.dot_general(
        samples,
        samples,
        (((0,), (0,)), ((), ())),
        precision=lax.Precision.HIGHEST,
        preferred_element_type=jnp.float32,
    )
    pivot_sub = pivot_rows // full_width
    pivot_dof = pivot_rows % full_width
    holder = (pivot_sub // sub_local == sub_place) & (pivot_dof // group == iface_place)
    local_row = pivot_sub % sub_local * group + pivot_dof % group
    picked_part = jnp.take(samples, local_row, axis=0, mode="clip").T * holder[None, :].astype(
        jnp.float32
    )
    partial = jnp.concatenate((gram_part, picked_part), axis=1)[None]
    total = group_sum(group_sum(partial[0], "sub", sub_count), "iface", iface_count)
    gram_matrix = total[:, :sample_count]
    picked = total[:, sample_count:]
    total_rows = float(sub_local * sub_count * full_width)
    coefficients = combine_weights(gram_matrix, picked, total_rows, sample_count)
    constraint_rows = lax.dot_general(
        coefficients,
        samples,
        (((1,), (1,)), ((), ())),
        precision=lax.Precision.HIGH,
        preferred_element_type=jnp.float32,
    )
    return constraint_rows.reshape(sample_count, sub_local, group)


def solution(mesh):
    placed = (
        P("sub", "iface", None),
        P(None, "sub", "iface"),
        P("sub", "iface"),
        P("sub", "iface"),
        P(),
    )
    return jax.shard_map(
        shards, mesh=mesh, in_specs=placed, out_specs=P(None, "sub", "iface"), check_vma=False
    )
```

```python
import functools
import math

import jax
import jax.numpy as jnp
from jax import lax
from jax.experimental import pallas as pl
from jax.experimental.pallas import tpu as pltpu
from jax.sharding import PartitionSpec as P

UNROLL = 128


def _pack_kernel(slot_ref, *refs):
    x_refs, o_ref, buf = refs[:-2], refs[-2], refs[-1]
    offset = 0
    for x_ref in x_refs:
        def body(j, carry, x_ref=x_ref, offset=offset):
            base = pl.multiple_of(j * UNROLL, UNROLL)
            for u in range(UNROLL):
                buf[pl.ds(slot_ref[offset + base + u], 1), :] = x_ref[pl.ds(base + u, 1), :]
            return carry

        lax.fori_loop(0, x_ref.shape[0] // UNROLL, body, 0)
        offset += x_ref.shape[0]
    width = buf.shape[1]
    n, lanes = o_ref.shape
    per = lanes // width
    lane = lax.broadcasted_iota(jnp.int32, (n, lanes), 1) // width
    acc = jnp.zeros((n, lanes), jnp.float32)
    for t in range(per):
        piece = buf[pl.ds(t, n, stride=per), :]
        wide = jnp.concatenate([piece] + [jnp.zeros_like(piece)] * (per - 1), axis=1)
        if t:
            wide = pltpu.roll(wide, shift=width * t, axis=1)
        acc = jnp.where(lane == t, wide, acc)
    o_ref[...] = acc


def _unpack_kernel(first, count, src_ref, *refs):
    v_refs, inc_ref, o_ref, joined, picked = refs[:-4], refs[-4], refs[-3], refs[-2], refs[-1]
    rows = sum(v_ref.shape[0] for v_ref in v_refs)
    width = v_refs[0].shape[1]
    n, lanes = inc_ref.shape
    per = lanes // width
    offset = 0
    for v_ref in v_refs:
        joined[pl.ds(offset, v_ref.shape[0]), :] = v_ref[...]
        offset += v_ref.shape[0]
    inc = inc_ref[...]
    for t in range(per):
        part = inc if t == 0 else pltpu.roll(inc, shift=lanes - width * t, axis=1)
        joined[pl.ds(rows + t, n, stride=per), :] = part[:, :width]

    def body(j, carry):
        base = pl.multiple_of(j * UNROLL, UNROLL)
        for u in range(UNROLL):
            picked[pl.ds(base + u, 1), :] = joined[pl.ds(src_ref[first + base + u], 1), :]
        return carry

    lax.fori_loop(0, count // UNROLL, body, 0)
    offset = 0
    for v_ref in v_refs:
        low = max(offset, first)
        high = min(offset + v_ref.shape[0], first + count)
        if low < high:
            o_ref[pl.ds(low - first, high - low), :] = (
                v_ref[pl.ds(low - offset, high - low), :] - picked[pl.ds(low - first, high - low), :]
            )
        offset += v_ref.shape[0]


def pack_rows(xs, send_pos):
    rows = sum(x.shape[0] for x in xs)
    width = xs[0].shape[1]
    return pl.pallas_call(
        _pack_kernel,
        in_specs=[pl.BlockSpec(memory_space=pltpu.SMEM)]
        + [pl.BlockSpec(memory_space=pltpu.VMEM)] * len(xs),
        out_specs=pl.BlockSpec(memory_space=pltpu.VMEM),
        out_shape=jax.ShapeDtypeStruct((rows * width // 128, 128), xs[0].dtype),
        scratch_shapes=[pltpu.VMEM((rows + 8, width), xs[0].dtype)],
        compiler_params=pltpu.CompilerParams(vmem_limit_bytes=48 * 1024 * 1024),
    )(send_pos, *xs)


def unpack_jump(vs, incoming, source, first, count):
    rows = sum(v.shape[0] for v in vs)
    width = vs[0].shape[1]
    return pl.pallas_call(
        functools.partial(_unpack_kernel, first, count),
        in_specs=[pl.BlockSpec(memory_space=pltpu.SMEM)]
        + [pl.BlockSpec(memory_space=pltpu.VMEM)] * (len(vs) + 1),
        out_specs=pl.BlockSpec(memory_space=pltpu.VMEM),
        out_shape=jax.ShapeDtypeStruct((count, width), vs[0].dtype),
        scratch_shapes=[
            pltpu.VMEM((2 * rows, width), vs[0].dtype),
            pltpu.VMEM((count, width), vs[0].dtype),
        ],
        compiler_params=pltpu.CompilerParams(vmem_limit_bytes=48 * 1024 * 1024),
    )(source, *vs, incoming)


def exchange(parts, send_pos):
    outgoing = pack_rows(parts, send_pos)
    return lax.all_to_all(outgoing, ("iface", "sub"), split_axis=0, concat_axis=0, tiled=True)


def apply_blocks(jump_rows, schur_blocks, sub_local, group):
    width = jump_rows.shape[1]
    half = jump_rows.astype(jnp.bfloat16).reshape(sub_local, group, width).transpose(2, 0, 1)
    ring = lax.axis_size("iface")
    here = lax.axis_index("iface")

    def shifted(value, shift):
        return lax.ppermute(value, "iface", [(i, (i + shift) % ring) for i in range(ring)])

    def product(block, owner):
        columns = lax.dynamic_slice_in_dim(schur_blocks, owner * group, group, axis=2)
        return jnp.einsum("src,ksc->srk", columns, block, preferred_element_type=jnp.float32)

    if ring == 4:
        from_left = shifted(half, 1)
        from_right = shifted(half, ring - 1)
        split = width // 2
        far = jnp.concatenate(
            (shifted(from_left[:split], 1), shifted(from_right[split:], ring - 1)), axis=0
        )
        total = product(half, here)
        total = total + product(from_left, (here + ring - 1) % ring)
        total = total + product(from_right, (here + 1) % ring)
        total = total + product(far, (here + 2) % ring)
    else:
        total = None
        for shift in range(ring):
            block = shifted(half, shift) if shift else half
            part = product(block, (here - shift) % ring)
            total = part if total is None else total + part
    return total.reshape(sub_local * group, width)


def combine_weights(gram_matrix, picked, total_rows, sample_count):
    lower = jnp.linalg.cholesky(gram_matrix)
    solved = jax.scipy.linalg.cho_solve((lower, True), picked)
    coupling = jnp.dot(picked.T, solved, precision=lax.Precision.HIGHEST) * (
        total_rows / sample_count
    ) + jnp.eye(sample_count, dtype=jnp.float32)
    lower_two = jnp.linalg.cholesky(coupling)
    return jax.scipy.linalg.cho_solve((lower_two, True), solved.T) * (
        total_rows / math.sqrt(sample_count)
    )


def group_sum(x, axis, size):
    place = lax.axis_index(axis)
    bit = 1
    while bit < size:
        radix = min(4, size // bit)
        got = [x] + [
            lax.ppermute(x, axis, [(i, i ^ (m * bit)) for i in range(size)])
            for m in range(1, radix)
        ]
        stacked = jnp.stack(got)
        digit = (place // bit) % radix
        total = None
        for j in range(radix):
            term = stacked[jnp.bitwise_xor(digit, j)]
            total = term if total is None else total + term
        x = total
        bit *= radix
    return x


def shards(schur_blocks, noise_field, peer_device, partner_slot, pivot_rows):
    sample_count, sub_local, group = noise_field.shape
    row_count = sub_local * group
    iface_count = lax.axis_size("iface")
    sub_count = lax.axis_size("sub")
    device_count = iface_count * sub_count
    capacity = row_count // device_count
    full_width = group * iface_count
    iface_place = lax.axis_index("iface")
    sub_place = lax.axis_index("sub")
    device_self = iface_place * sub_count + sub_place
    peer_flat = peer_device.reshape(row_count)
    slot_flat = partner_slot.reshape(row_count)
    crossing = peer_flat != device_self
    send_pos = jnp.clip(
        jnp.where(crossing, peer_flat * capacity + slot_flat, row_count), 0, row_count
    ).astype(jnp.int32)
    source = jnp.clip(
        jnp.where(crossing, row_count + peer_flat * capacity + slot_flat, slot_flat),
        0,
        2 * row_count - 1,
    ).astype(jnp.int32)
    routing = (send_pos, source)
    noise_rows = noise_field.transpose(1, 2, 0).reshape(row_count, sample_count)
    field = [noise_rows]
    for _ in range(2):
        incoming = exchange(field, send_pos)
        jumped = unpack_jump(field, incoming, source, 0, row_count)
        field = [apply_blocks(jumped, schur_blocks, sub_local, group)]
    incoming = exchange(field, send_pos)
    samples = unpack_jump(field, incoming, source, 0, row_count)
    gram_part = lax.dot_general(
        samples,
        samples,
        (((0,), (0,)), ((), ())),
        precision=lax.Precision.HIGHEST,
        preferred_element_type=jnp.float32,
    )
    pivot_sub = pivot_rows // full_width
    pivot_dof = pivot_rows % full_width
    holder = (pivot_sub // sub_local == sub_place) & (pivot_dof // group == iface_place)
    local_row = pivot_sub % sub_local * group + pivot_dof % group
    picked_part = jnp.take(samples, local_row, axis=0, mode="clip").T * holder[None, :].astype(
        jnp.float32
    )
    partial = jnp.concatenate((gram_part, picked_part), axis=1)[None]
    total = group_sum(group_sum(partial[0], "sub", sub_count), "iface", iface_count)
    gram_matrix = total[:, :sample_count]
    picked = total[:, sample_count:]
    total_rows = float(sub_local * sub_count * full_width)
    coefficients = combine_weights(gram_matrix, picked, total_rows, sample_count)
    constraint_rows = lax.dot_general(
        coefficients,
        samples,
        (((1,), (1,)), ((), ())),
        precision=lax.Precision.HIGH,
        preferred_element_type=jnp.float32,
    )
    return constraint_rows.reshape(sample_count, sub_local, group)


def solution(mesh):
    placed = (
        P("sub", "iface", None),
        P(None, "sub", "iface"),
        P("sub", "iface"),
        P("sub", "iface"),
        P(),
    )
    return jax.shard_map(
        shards, mesh=mesh, in_specs=placed, out_specs=P(None, "sub", "iface"), check_vma=False
    )
```
